512 devices in a mesh: dp: 4 (over z_hi, core), tm: 8 (over z_lo), height: 16 (over x, y).
Axes of the slice: x: 4, y: 4, z: 16 (z_hi: 2, z_lo: 8; z = z_hi * 8 + z_lo), core: 2. Of those that a mesh axis runs over, the one named last changes fastest.
Arguments:
- clips: bfloat16 [4, 16, 64, 128, 128], P('dp', 'tm', 'height'), may hold values from -6 to 6
- frame_counts: int32 [4, 5], P('dp'), may hold values from 1 to 9, 16 in all within a row
- conv_first: bfloat16 [3, 3, 3, 128, 128], replicated, may hold values from -0.109375 to 0.109375
- conv_down: bfloat16 [3, 3, 3, 128, 128], replicated, may hold values from -0.109375 to 0.109375
- out_cotangent: bfloat16 [4, 8, 32, 64, 128], P('dp', 'tm', 'height'), may hold values from -6 to 6
Outputs:
- encoded: bfloat16 [4, 8, 32, 64, 128], P('dp', 'tm', 'height')
- grad_first: bfloat16 [3, 3, 3, 128, 128], P(None, None, None, 'dp')
- grad_down: bfloat16 [3, 3, 3, 128, 128], P(None, None, None, 'dp')
The draws below stay inside these ranges and needn't reach their ends.
Inputs may be any that keep to these rules, and one draw needn't show every extreme that they name: `frame_counts`: each sequence's 5 clip lengths sum to 16; in every sequence one clip has exactly 9 frames.
All inputs are finite; a program needn't handle non-finite values.
Results may differ from the reference program's by a relative error of at most 0.0059.
Values may be sent and summed in bfloat16 or wider, within the bound.
No kernel may reach another device: no remote copies, remote signals or barrier semaphores. Data moves between devices by JAX's collectives and lax.ppermute only.
A program may use at most 64 MiB of HBM per device.

```python
import math
import jax
import jax.numpy as jnp
import numpy as np
from jax import lax

C = 128
WIDE = 128
SEQS = 4
FRAMES = 16
ROWS = 64
CLIPS = 5
MOST = 9


def shard_levels(own_key, extent, shards, smallest, high):
    loudness = 1.0
    for axis_at, blocks in shards:
        heights = jax.random.uniform(jax.random.fold_in(jax.random.fold_in(own_key, 6), axis_at), (blocks,), jnp.float32, smallest / len(shards), high / len(shards))
        loudness = loudness * jnp.repeat(jnp.exp(heights), extent[axis_at] // blocks).reshape((-1,) + (1,) * (len(extent) - 1 - axis_at))
    return loudness


def length_profile(count, total, limit, slope):
    portions = [(1 << 20) // math.isqrt(grade ** slope) + 1 for grade in range(2, count + 1)]
    surplus, given = total - limit - (count - 1), [1] * (count - 1)
    while surplus > 0:
        candidates = [i for i in range(count - 1) if given[i] < limit]
        mass, remaining = sum([portions[i] for i in candidates]), surplus
        for i in candidates:
            extra = min(limit - given[i], max(1, remaining * portions[i] // mass), surplus)
            given[i] = given[i] + extra
            surplus = surplus - extra
    return np.array([limit] + given)


def ragged_sizes(stream_key, number_of, total, most, slope):
    if number_of == 2:
        one = jax.random.randint(stream_key, (), max(1, total - most), min(most, total - 1) + 1)
        return jnp.stack([one, total - one])
    tallies = jnp.asarray(length_profile(number_of, total, most, slope), jnp.int32)
    couples = (number_of - 1) // 2
    giver, sink = tallies[1:1 + 2 * couples:2], tallies[2:2 + 2 * couples:2]
    slack = jnp.minimum(giver - 1, most - sink)
    passed = jax.random.randint(jax.random.fold_in(stream_key, 1), (couples,), 0, 1 << 20) % (slack + 1)
    tallies = tallies.at[1:1 + 2 * couples:2].set(giver - passed).at[2:2 + 2 * couples:2].set(sink + passed)
    return tallies[jax.random.permutation(jax.random.fold_in(stream_key, 2), number_of)]


def gaussian(stream_key, dims, scale, limit, split=(), held_as=jnp.bfloat16):
    factor_of = shard_levels(stream_key, dims, split, -0.22, 0.18) if split else 1.0
    result = jax.random.normal(stream_key, dims, jnp.float32) * scale * factor_of
    return jnp.minimum(jnp.maximum(result, -limit), limit).astype(held_as)


def setup_inputs(seed: int = 0) -> dict:
    key_of = jax.random.split(jax.random.key(seed), 6)
    return {
        "clips": gaussian(key_of[0], (SEQS, FRAMES, ROWS, WIDE, C), 1.0, 6.0, ((0, 4), (1, 8), (2, 16))),
        "frame_counts": jax.vmap(lambda own: ragged_sizes(own, CLIPS, FRAMES, MOST, 2))(jax.random.split(key_of[1], SEQS)).reshape((SEQS, CLIPS)).astype(jnp.int32),
        "conv_first": gaussian(key_of[2], (3, 3, 3, C, C), (27 * C) ** -0.5, 0.109375),
        "conv_down": gaussian(key_of[3], (3, 3, 3, C, C), (27 * C) ** -0.5, 0.109375),
        "out_cotangent": gaussian(key_of[4], (SEQS, FRAMES // 2, ROWS // 2, WIDE // 2, C), 1.0, 6.0, ((0, 4), (1, 8), (2, 16))),
    }


def unfold(frame_slab, stride, pad_cols):
    padded = jnp.pad(frame_slab, ((0, 0), (0, 0), pad_cols, (0, 0)))
    out_rows = (padded.shape[1] - 3) // stride + 1
    out_cols = (padded.shape[2] - 3) // stride + 1
    pieces = []
    for tap_row in range(3):
        for tap_col in range(3):
            pieces.append(padded[:, tap_row:tap_row + stride * (out_rows - 1) + 1:stride, tap_col:tap_col + stride * (out_cols - 1) + 1:stride])
    joined = jnp.concatenate(pieces, axis=-1)
    return (joined.reshape(-1, joined.shape[-1]), (frame_slab.shape[0], out_rows, out_cols))

def conv_layer(extended, weight, tap_mask, out_frames, stride, pad_cols):
    channels_out = weight.shape[-1]
    summed = None
    for tap_time in range(3):
        frame_slab = extended[tap_time:tap_time + stride * (out_frames - 1) + 1:stride]
        columns, shape_out = unfold(frame_slab, stride, pad_cols)
        kernel = weight[tap_time].reshape(-1, channels_out)
        tap_term = jnp.dot(columns, kernel, preferred_element_type=jnp.float32).reshape(shape_out + (channels_out,))
        tap_term = tap_term * tap_mask[:, tap_time][:, None, None, None]
        summed = tap_term if summed is None else summed + tap_term
    return summed

def weight_grad(extended, grads, tap_mask, stride, pad_cols):
    out_frames = grads.shape[0]
    blocks = []
    for tap_time in range(3):
        frame_slab = extended[tap_time:tap_time + stride * (out_frames - 1) + 1:stride]
        columns, shape_out = unfold(frame_slab, stride, pad_cols)
        masked = grads * tap_mask[:, tap_time].astype(jnp.bfloat16)[:, None, None, None]
        blocks.append(jnp.dot(columns.T, masked.reshape(-1, grads.shape[-1]), preferred_element_type=jnp.float32))
    stacked = jnp.stack(blocks)
    return stacked.reshape(3, 3, 3, extended.shape[-1], grads.shape[-1])

def hidden_grad(grads_ext, weight, mask_ext):
    pieces = []
    for tap_time in range(3):
        masked = grads_ext * mask_ext[:, tap_time].astype(jnp.bfloat16)[:, None, None, None]
        kernel = jnp.transpose(weight[tap_time][::-1, ::-1], (0, 1, 3, 2))
        spread = lax.conv_general_dilated(masked, kernel, (1, 1), ((2, 0), (2, 2)), lhs_dilation=(2, 2), dimension_numbers=('NHWC', 'HWIO', 'NHWC'), preferred_element_type=jnp.float32)
        pieces.append(spread[:, 1:, 1:])
    even_frames = pieces[2][:-1] + pieces[0][1:]
    odd_frames = pieces[1][1:]
    merged = jnp.stack([even_frames, odd_frames], axis=1)
    return merged.reshape((2 * even_frames.shape[0],) + even_frames.shape[1:])

def positions(counts_row, frame_index):
    starts = (jnp.cumsum(counts_row) - counts_row).astype(jnp.int32)
    latest = lax.optimization_barrier(jnp.max(jnp.where(starts[None, :] <= frame_index[:, None], starts[None, :], 0), axis=1))
    return (frame_index - latest).astype(jnp.int32)

def tap_masks(place):
    return (place[:, None] >= (2 - jnp.arange(3, dtype=jnp.int32))[None, :]).astype(jnp.float32)

def reference(clips, frame_counts, conv_first, conv_down, out_cotangent):
    scale = 1.0 / math.sqrt(SEQS * (FRAMES // 2) * (ROWS // 2) * (WIDE // 2))
    encoded_list = []
    first_sum = jnp.zeros(conv_first.shape, jnp.float32)
    down_sum = jnp.zeros(conv_down.shape, jnp.float32)
    for sequence in range(SEQS):
        frame_index = jnp.arange(FRAMES, dtype=jnp.int32)
        place = positions(frame_counts[sequence], frame_index)
        first_mask = tap_masks(place)
        down_mask = tap_masks(place[0::2])
        input_ext = jnp.pad(clips[sequence], ((2, 0), (1, 1), (0, 0), (0, 0)))
        pre_act = conv_layer(input_ext, conv_first, first_mask, FRAMES, 1, (1, 1))
        hidden = jax.nn.silu(pre_act).astype(jnp.bfloat16)
        hidden_ext = jnp.pad(hidden, ((2, 0), (1, 0), (0, 0), (0, 0)))
        encoded_list.append(conv_layer(hidden_ext, conv_down, down_mask, FRAMES // 2, 2, (1, 0)).astype(jnp.bfloat16))
        grads = (out_cotangent[sequence].astype(jnp.float32) * scale).astype(jnp.bfloat16)
        down_sum = down_sum + weight_grad(hidden_ext, grads, down_mask, 2, (1, 0))
        grads_ext = jnp.pad(grads, ((0, 1), (0, 1), (0, 0), (0, 0)))
        mask_ext = jnp.concatenate([down_mask, jnp.ones((1, 3), jnp.float32)], axis=0)
        back_hidden = hidden_grad(grads_ext, conv_down, mask_ext).astype(jnp.bfloat16)
        sigma = jax.nn.sigmoid(pre_act)
        pre_grad = (back_hidden.astype(jnp.float32) * sigma * (1.0 + pre_act * (1.0 - sigma))).astype(jnp.bfloat16)
        first_sum = first_sum + weight_grad(input_ext, pre_grad, first_mask, 1, (1, 1))
    return (jnp.stack(encoded_list), first_sum.astype(jnp.bfloat16), down_sum.astype(jnp.bfloat16))
```

```python
import math

import jax
import jax.numpy as jnp
from jax import lax
from jax.sharding import PartitionSpec as P


def padded_2(cells, sides, width):
    for axis, dim in sides:
        count = lax.axis_size(axis)
        ends = count - 1
        head = lax.slice_in_dim(cells, 0, width, axis=dim)
        tail = lax.slice_in_dim(cells, cells.shape[dim] - width, cells.shape[dim], axis=dim)
        cells = jnp.concatenate(
            [
                lax.ppermute(tail, axis, [(i, (i + 1) % count) for i in range(ends)]),
                cells,
                lax.ppermute(head, axis, [((i + 1) % count, i) for i in range(ends)]),
            ],
            axis=dim,
        )
    return cells


def shifted(value, axis, steps):
    count = lax.axis_size(axis)
    leading, last = (max(0, -steps), min(count, count - steps))
    return lax.ppermute(value, axis, [(source, source + steps) for source in range(leading, last)])


def unfold(frame_slab, stride, pad_cols):
    padded = jnp.pad(frame_slab, ((0, 0), (0, 0), pad_cols, (0, 0)))
    out_rows = (padded.shape[1] - 3) // stride + 1
    out_cols = (padded.shape[2] - 3) // stride + 1
    pieces = []
    for tap_row in range(3):
        for tap_col in range(3):
            pieces.append(
                padded[
                    :,
                    tap_row : tap_row + stride * (out_rows - 1) + 1 : stride,
                    tap_col : tap_col + stride * (out_cols - 1) + 1 : stride,
                ]
            )
    joined = jnp.concatenate(pieces, axis=-1)
    return (joined.reshape(-1, joined.shape[-1]), (frame_slab.shape[0], out_rows, out_cols))


def conv_layer(extended, weight, tap_mask, out_frames, stride, pad_cols):
    channels_out = weight.shape[-1]
    summed = None
    for tap_time in range(3):
        frame_slab = extended[tap_time : tap_time + stride * (out_frames - 1) + 1 : stride]
        columns, shape_out = unfold(frame_slab, stride, pad_cols)
        kernel = weight[tap_time].reshape(-1, channels_out)
        tap_term = jnp.dot(columns, kernel, preferred_element_type=jnp.float32).reshape(
            shape_out + (channels_out,)
        )
        tap_term = tap_term * tap_mask[:, tap_time][:, None, None, None]
        summed = tap_term if summed is None else summed + tap_term
    return summed


def weight_grad(extended, grads, tap_mask, stride, pad_cols):
    out_frames = grads.shape[0]
    blocks = []
    for tap_time in range(3):
        frame_slab = extended[tap_time : tap_time + stride * (out_frames - 1) + 1 : stride]
        columns, shape_out = unfold(frame_slab, stride, pad_cols)
        masked = grads * tap_mask[:, tap_time].astype(jnp.bfloat16)[:, None, None, None]
        blocks.append(
            jnp.dot(
                columns.T, masked.reshape(-1, grads.shape[-1]), preferred_element_type=jnp.float32
            )
        )
    stacked = jnp.stack(blocks)
    return stacked.reshape(3, 3, 3, extended.shape[-1], grads.shape[-1])


def hidden_grad(grads_ext, weight, mask_ext):
    pieces = []
    for tap_time in range(3):
        masked = grads_ext * mask_ext[:, tap_time].astype(jnp.bfloat16)[:, None, None, None]
        kernel = jnp.transpose(weight[tap_time][::-1, ::-1], (0, 1, 3, 2))
        spread = lax.conv_general_dilated(
            masked,
            kernel,
            (1, 1),
            ((2, 0), (2, 2)),
            lhs_dilation=(2, 2),
            dimension_numbers=("NHWC", "HWIO", "NHWC"),
            preferred_element_type=jnp.float32,
        )
        pieces.append(spread[:, 1:, 1:])
    even_frames = pieces[2][:-1] + pieces[0][1:]
    odd_frames = pieces[1][1:]
    merged = jnp.stack([even_frames, odd_frames], axis=1)
    return merged.reshape((2 * even_frames.shape[0],) + even_frames.shape[1:])


def positions(counts_row, frame_index):
    starts = jnp.cumsum(counts_row) - counts_row
    latest = jnp.max(jnp.where(starts[None, :] <= frame_index[:, None], starts[None, :], 0), axis=1)
    return frame_index - latest


def tap_masks(place):
    return (place[:, None] >= (2 - jnp.arange(3, dtype=jnp.int32))[None, :]).astype(jnp.float32)


def body(clips, frame_counts, conv_first, conv_down, out_cotangent):
    frames_dev = clips.shape[1]
    rows_dev = clips.shape[2]
    columns_all = clips.shape[3]
    down_frames = frames_dev // 2
    counts_row = frame_counts[0]
    first_frame = lax.axis_index("tm") * frames_dev
    frame_index = first_frame + jnp.arange(frames_dev, dtype=jnp.int32)
    first_mask = tap_masks(positions(counts_row, frame_index))
    down_index = first_frame + 2 * jnp.arange(down_frames + 1, dtype=jnp.int32)
    mask_ext = tap_masks(positions(counts_row, down_index))
    down_mask = mask_ext[:down_frames]
    with_rows = padded_2(clips[0], (("height", 1),), 1)
    earlier = shifted(with_rows, "tm", 1)
    input_ext = jnp.concatenate([earlier, with_rows], axis=0)
    pre_act = conv_layer(input_ext, conv_first, first_mask, frames_dev, 1, (1, 1))
    hidden = jax.nn.silu(pre_act).astype(jnp.bfloat16)
    above = shifted(hidden[:, rows_dev - 1 :], "height", 1)
    hidden_rows = jnp.concatenate([above, hidden], axis=1)
    hidden_past = shifted(hidden_rows, "tm", 1)
    hidden_ext = jnp.concatenate([hidden_past, hidden_rows], axis=0)
    encoded = conv_layer(hidden_ext, conv_down, down_mask, down_frames, 2, (1, 0)).astype(
        jnp.bfloat16
    )
    cells_all = (
        lax.axis_size("dp")
        * clips.shape[0]
        * down_frames
        * lax.axis_size("tm")
        * (rows_dev // 2)
        * lax.axis_size("height")
        * (columns_all // 2)
    )
    scale = 1.0 / math.sqrt(cells_all)
    grads = (out_cotangent[0].astype(jnp.float32) * scale).astype(jnp.bfloat16)
    down_local = weight_grad(hidden_ext, grads, down_mask, 2, (1, 0))
    below = shifted(grads[:, 0:1], "height", -1)
    grads_rows = jnp.concatenate([grads, below], axis=1)
    grads_next = shifted(grads_rows, "tm", -1)
    grads_ext = jnp.concatenate([grads_rows, grads_next], axis=0)
    back_hidden = hidden_grad(grads_ext, conv_down, mask_ext).astype(jnp.bfloat16)
    sigma = jax.nn.sigmoid(pre_act)
    pre_grad = (back_hidden.astype(jnp.float32) * sigma * (1.0 + pre_act * (1.0 - sigma))).astype(
        jnp.bfloat16
    )
    first_local = weight_grad(input_ext, pre_grad, first_mask, 1, (1, 1))
    share = conv_first.shape[3] // lax.axis_size("dp")
    quarters = lax.axis_size("dp")

    def by_quarter(term):
        term = term.reshape(27, quarters, share, term.shape[-1])
        return jnp.transpose(term, (1, 0, 2, 3)).reshape(quarters, -1)

    stacked = jnp.concatenate([by_quarter(first_local), by_quarter(down_local)], axis=1)
    rows_n, frames_n = lax.axis_size("height"), lax.axis_size("tm")
    piece = stacked.reshape(quarters, rows_n, frames_n, -1)
    piece = lax.psum_scatter(piece, "height", scatter_dimension=1, tiled=True)
    piece = lax.psum_scatter(piece, "tm", scatter_dimension=2, tiled=True)
    piece = lax.psum_scatter(piece, "dp", scatter_dimension=0, tiled=True)
    piece = piece.astype(jnp.bfloat16)
    piece = lax.all_gather(piece, "tm", axis=2, tiled=True)
    gathered = lax.all_gather(piece, "height", axis=1, tiled=True).reshape(-1)
    half = gathered.shape[0] // 2
    kernel_shape = (3, 3, 3, share, conv_first.shape[-1])
    summed_first = gathered[:half].reshape(kernel_shape)
    summed_down = gathered[half:].reshape(kernel_shape)
    return (encoded[None], summed_first, summed_down)


def solution(mesh):
    in_specs = (
        P("dp", "tm", "height", None, None),
        P("dp", None),
        P(),
        P(),
        P("dp", "tm", "height", None, None),
    )
    out_specs = (
        P("dp", "tm", "height", None, None),
        P(None, None, None, "dp", None),
        P(None, None, None, "dp", None),
    )
    return jax.shard_map(body, mesh=mesh, in_specs=in_specs, out_specs=out_specs, check_vma=False)
```

```python
import math

import jax
import jax.numpy as jnp
from jax import lax
from jax.sharding import PartitionSpec as P


def padded_2(cells, sides, width):
    for axis, dim in sides:
        count = lax.axis_size(axis)
        ends = count - 1
        head = lax.slice_in_dim(cells, 0, width, axis=dim)
        tail = lax.slice_in_dim(cells, cells.shape[dim] - width, cells.shape[dim], axis=dim)
        cells = jnp.concatenate(
            [
                lax.ppermute(tail, axis, [(i, (i + 1) % count) for i in range(ends)]),
                cells,
                lax.ppermute(head, axis, [((i + 1) % count, i) for i in range(ends)]),
            ],
            axis=dim,
        )
    return cells


def shifted(value, axis, steps):
    count = lax.axis_size(axis)
    leading, last = (max(0, -steps), min(count, count - steps))
    return lax.ppermute(value, axis, [(source, source + steps) for source in range(leading, last)])


def unfold(frame_slab, stride, pad_cols):
    padded = jnp.pad(frame_slab, ((0, 0), (0, 0), pad_cols, (0, 0)))
    out_rows = (padded.shape[1] - 3) // stride + 1
    out_cols = (padded.shape[2] - 3) // stride + 1
    pieces = []
    for tap_row in range(3):
        for tap_col in range(3):
            pieces.append(
                padded[
                    :,
                    tap_row : tap_row + stride * (out_rows - 1) + 1 : stride,
                    tap_col : tap_col + stride * (out_cols - 1) + 1 : stride,
                ]
            )
    joined = jnp.concatenate(pieces, axis=-1)
    return (joined.reshape(-1, joined.shape[-1]), (frame_slab.shape[0], out_rows, out_cols))


def conv_layer(extended, weight, tap_mask, out_frames, stride, pad_cols):
    channels_out = weight.shape[-1]
    summed = None
    for tap_time in range(3):
        frame_slab = extended[tap_time : tap_time + stride * (out_frames - 1) + 1 : stride]
        columns, shape_out = unfold(frame_slab, stride, pad_cols)
        kernel = weight[tap_time].reshape(-1, channels_out)
        tap_term = jnp.dot(columns, kernel, preferred_element_type=jnp.float32).reshape(
            shape_out + (channels_out,)
        )
        tap_term = tap_term * tap_mask[:, tap_time][:, None, None, None]
        summed = tap_term if summed is None else summed + tap_term
    return summed


def weight_grad(extended, grads, tap_mask, stride, pad_cols):
    out_frames = grads.shape[0]
    blocks = []
    for tap_time in range(3):
        frame_slab = extended[tap_time : tap_time + stride * (out_frames - 1) + 1 : stride]
        columns, shape_out = unfold(frame_slab, stride, pad_cols)
        masked = grads * tap_mask[:, tap_time].astype(jnp.bfloat16)[:, None, None, None]
        blocks.append(
            jnp.dot(
                columns.T, masked.reshape(-1, grads.shape[-1]), preferred_element_type=jnp.float32
            )
        )
    stacked = jnp.stack(blocks)
    return stacked.reshape(3, 3, 3, extended.shape[-1], grads.shape[-1])


def hidden_grad(grads_ext, weight, mask_ext):
    pieces = []
    for tap_time in range(3):
        masked = grads_ext * mask_ext[:, tap_time].astype(jnp.bfloat16)[:, None, None, None]
        kernel = jnp.transpose(weight[tap_time][::-1, ::-1], (0, 1, 3, 2))
        spread = lax.conv_general_dilated(
            masked,
            kernel,
            (1, 1),
            ((2, 0), (2, 2)),
            lhs_dilation=(2, 2),
            dimension_numbers=("NHWC", "HWIO", "NHWC"),
            preferred_element_type=jnp.float32,
        )
        pieces.append(spread[:, 1:, 1:])
    even_frames = pieces[2][:-1] + pieces[0][1:]
    odd_frames = pieces[1][1:]
    merged = jnp.stack([even_frames, odd_frames], axis=1)
    return merged.reshape((2 * even_frames.shape[0],) + even_frames.shape[1:])


def positions(counts_row, frame_index):
    starts = jnp.cumsum(counts_row) - counts_row
    latest = jnp.max(jnp.where(starts[None, :] <= frame_index[:, None], starts[None, :], 0), axis=1)
    return frame_index - latest


def tap_masks(place):
    return (place[:, None] >= (2 - jnp.arange(3, dtype=jnp.int32))[None, :]).astype(jnp.float32)


def body(clips, frame_counts, conv_first, conv_down, out_cotangent):
    frames_dev = clips.shape[1]
    rows_dev = clips.shape[2]
    columns_all = clips.shape[3]
    down_frames = frames_dev // 2
    counts_row = frame_counts[0]
    first_frame = lax.axis_index("tm") * frames_dev
    frame_index = first_frame + jnp.arange(frames_dev, dtype=jnp.int32)
    first_mask = tap_masks(positions(counts_row, frame_index))
    down_index = first_frame + 2 * jnp.arange(down_frames + 1, dtype=jnp.int32)
    mask_ext = tap_masks(positions(counts_row, down_index))
    down_mask = mask_ext[:down_frames]
    with_rows = padded_2(clips[0], (("height", 1),), 1)
    earlier = shifted(with_rows, "tm", 1)
    input_ext = jnp.concatenate([earlier, with_rows], axis=0)
    pre_act = conv_layer(input_ext, conv_first, first_mask, frames_dev, 1, (1, 1))
    hidden = jax.nn.silu(pre_act).astype(jnp.bfloat16)
    above = shifted(hidden[:, rows_dev - 1 :], "height", 1)
    hidden_rows = jnp.concatenate([above, hidden], axis=1)
    hidden_past = shifted(hidden_rows, "tm", 1)
    hidden_ext = jnp.concatenate([hidden_past, hidden_rows], axis=0)
    encoded = conv_layer(hidden_ext, conv_down, down_mask, down_frames, 2, (1, 0)).astype(
        jnp.bfloat16
    )
    cells_all = (
        lax.axis_size("dp")
        * clips.shape[0]
        * down_frames
        * lax.axis_size("tm")
        * (rows_dev // 2)
        * lax.axis_size("height")
        * (columns_all // 2)
    )
    scale = 1.0 / math.sqrt(cells_all)
    grads = (out_cotangent[0].astype(jnp.float32) * scale).astype(jnp.bfloat16)
    down_local = weight_grad(hidden_ext, grads, down_mask, 2, (1, 0))
    below = shifted(grads[:, 0:1], "height", -1)
    grads_rows = jnp.concatenate([grads, below], axis=1)
    grads_next = shifted(grads_rows, "tm", -1)
    grads_ext = jnp.concatenate([grads_rows, grads_next], axis=0)
    back_hidden = hidden_grad(grads_ext, conv_down, mask_ext).astype(jnp.bfloat16)
    sigma = jax.nn.sigmoid(pre_act)
    pre_grad = (back_hidden.astype(jnp.float32) * sigma * (1.0 + pre_act * (1.0 - sigma))).astype(
        jnp.bfloat16
    )
    first_local = weight_grad(input_ext, pre_grad, first_mask, 1, (1, 1))
    share = conv_first.shape[3] // lax.axis_size("dp")
    quarters = lax.axis_size("dp")
    rows_n, frames_n = lax.axis_size("height"), lax.axis_size("tm")

    def by_quarter(term):
        term = term.reshape(27, quarters, share, term.shape[-1])
        return jnp.transpose(term, (1, 0, 2, 3)).reshape(quarters, -1)

    stacked = jnp.concatenate([by_quarter(first_local), by_quarter(down_local)], axis=1)
    owned = reduce_to_owner(stacked.reshape(quarters // 2, 2, rows_n, frames_n, -1))
    piece = owned.astype(jnp.bfloat16)
    piece = gather_ring(piece, "tm")
    gathered = gather_ring(piece, "height").reshape(-1)
    half = gathered.shape[0] // 2
    kernel_shape = (3, 3, 3, share, conv_first.shape[-1])
    summed_first = gathered[:half].reshape(kernel_shape)
    summed_down = gathered[half:].reshape(kernel_shape)
    return (encoded[None], summed_first, summed_down)


def pair_swap(value, axis, bit):
    count = lax.axis_size(axis)
    return lax.ppermute(value, axis, [(i, i ^ bit) for i in range(count)])


def scatter_axis(blocks, axis):
    count = lax.axis_size(axis)
    me = lax.axis_index(axis)
    total = lax.dynamic_index_in_dim(blocks, me, 0, keepdims=False)
    for step in range(1, count):
        sent = lax.dynamic_index_in_dim(blocks, (me + step) % count, 0, keepdims=False)
        total = total + lax.ppermute(sent, axis, [(i, (i + step) % count) for i in range(count)])
    return total


def reduce_to_owner(blocks):
    core = lax.axis_index("dp") % 2
    mine = lax.dynamic_index_in_dim(blocks, core, 1, keepdims=False)
    other = lax.dynamic_index_in_dim(blocks, 1 - core, 1, keepdims=False)
    blocks = mine + pair_swap(other, "dp", 1)
    blocks = jnp.moveaxis(blocks, 1, 0)
    blocks = scatter_axis(blocks, "height")
    blocks = jnp.moveaxis(blocks, 1, 0)
    blocks = scatter_axis(blocks, "tm")
    far = lax.axis_index("dp") // 2
    mine = lax.dynamic_index_in_dim(blocks, far, 0, keepdims=False)
    other = lax.dynamic_index_in_dim(blocks, 1 - far, 0, keepdims=False)
    return mine + pair_swap(other, "dp", 2)


def gather_ring(piece, axis):
    count = lax.axis_size(axis)
    me = lax.axis_index(axis)
    received = [piece]
    for step in range(1, count):
        received.append(lax.ppermute(piece, axis, [(i, (i + step) % count) for i in range(count)]))
    stacked = jnp.stack(received)
    order = (me - jnp.arange(count, dtype=jnp.int32)) % count
    return stacked[order]


def solution(mesh):
    in_specs = (
        P("dp", "tm", "height", None, None),
        P("dp", None),
        P(),
        P(),
        P("dp", "tm", "height", None, None),
    )
    out_specs = (
        P("dp", "tm", "height", None, None),
        P(None, None, None, "dp", None),
        P(None, None, None, "dp", None),
    )
    return jax.shard_map(body, mesh=mesh, in_specs=in_specs, out_specs=out_specs, check_vma=False)
```

```python
import math

import jax
import jax.numpy as jnp
from jax import lax
from jax.sharding import PartitionSpec as P


def padded_2(cells, sides, width):
    for axis, dim in sides:
        count = lax.axis_size(axis)
        ends = count - 1
        head = lax.slice_in_dim(cells, 0, width, axis=dim)
        tail = lax.slice_in_dim(cells, cells.shape[dim] - width, cells.shape[dim], axis=dim)
        cells = jnp.concatenate(
            [
                lax.ppermute(tail, axis, [(i, (i + 1) % count) for i in range(ends)]),
                cells,
                lax.ppermute(head, axis, [((i + 1) % count, i) for i in range(ends)]),
            ],
            axis=dim,
        )
    return cells


def shifted(value, axis, steps):
    count = lax.axis_size(axis)
    leading, last = (max(0, -steps), min(count, count - steps))
    return lax.ppermute(value, axis, [(source, source + steps) for source in range(leading, last)])


def unfold(frame_slab, stride, pad_cols):
    padded = jnp.pad(frame_slab, ((0, 0), (0, 0), pad_cols, (0, 0)))
    out_rows = (padded.shape[1] - 3) // stride + 1
    out_cols = (padded.shape[2] - 3) // stride + 1
    pieces = []
    for tap_row in range(3):
        for tap_col in range(3):
            pieces.append(
                padded[
                    :,
                    tap_row : tap_row + stride * (out_rows - 1) + 1 : stride,
                    tap_col : tap_col + stride * (out_cols - 1) + 1 : stride,
                ]
            )
    joined = jnp.concatenate(pieces, axis=-1)
    return (joined.reshape(-1, joined.shape[-1]), (frame_slab.shape[0], out_rows, out_cols))


def conv_layer(extended, weight, tap_mask, out_frames, stride, pad_cols):
    channels_out = weight.shape[-1]
    summed = None
    for tap_time in range(3):
        frame_slab = extended[tap_time : tap_time + stride * (out_frames - 1) + 1 : stride]
        columns, shape_out = unfold(frame_slab, stride, pad_cols)
        kernel = weight[tap_time].reshape(-1, channels_out)
        tap_term = jnp.dot(columns, kernel, preferred_element_type=jnp.float32).reshape(
            shape_out + (channels_out,)
        )
        tap_term = tap_term * tap_mask[:, tap_time][:, None, None, None]
        summed = tap_term if summed is None else summed + tap_term
    return summed


def weight_grad(extended, grads, tap_mask, stride, pad_cols):
    out_frames = grads.shape[0]
    blocks = []
    for tap_time in range(3):
        frame_slab = extended[tap_time : tap_time + stride * (out_frames - 1) + 1 : stride]
        columns, shape_out = unfold(frame_slab, stride, pad_cols)
        masked = grads * tap_mask[:, tap_time].astype(jnp.bfloat16)[:, None, None, None]
        blocks.append(
            jnp.dot(
                columns.T, masked.reshape(-1, grads.shape[-1]), preferred_element_type=jnp.float32
            )
        )
    stacked = jnp.stack(blocks)
    return stacked.reshape(3, 3, 3, extended.shape[-1], grads.shape[-1])


def hidden_grad(grads_ext, weight, mask_ext):
    pieces = []
    for tap_time in range(3):
        masked = grads_ext * mask_ext[:, tap_time].astype(jnp.bfloat16)[:, None, None, None]
        kernel = jnp.transpose(weight[tap_time][::-1, ::-1], (0, 1, 3, 2))
        spread = lax.conv_general_dilated(
            masked,
            kernel,
            (1, 1),
            ((2, 0), (2, 2)),
            lhs_dilation=(2, 2),
            dimension_numbers=("NHWC", "HWIO", "NHWC"),
            preferred_element_type=jnp.float32,
        )
        pieces.append(spread[:, 1:, 1:])
    even_frames = pieces[2][:-1] + pieces[0][1:]
    odd_frames = pieces[1][1:]
    merged = jnp.stack([even_frames, odd_frames], axis=1)
    return merged.reshape((2 * even_frames.shape[0],) + even_frames.shape[1:])


def positions(counts_row, frame_index):
    starts = jnp.cumsum(counts_row) - counts_row
    latest = jnp.max(jnp.where(starts[None, :] <= frame_index[:, None], starts[None, :], 0), axis=1)
    return frame_index - latest


def tap_masks(place):
    return (place[:, None] >= (2 - jnp.arange(3, dtype=jnp.int32))[None, :]).astype(jnp.float32)


def body(clips, frame_counts, conv_first, conv_down, out_cotangent):
    frames_dev = clips.shape[1]
    rows_dev = clips.shape[2]
    columns_all = clips.shape[3]
    down_frames = frames_dev // 2
    counts_row = frame_counts[0]
    first_frame = lax.axis_index("tm") * frames_dev
    frame_index = first_frame + jnp.arange(frames_dev, dtype=jnp.int32)
    first_mask = tap_masks(positions(counts_row, frame_index))
    down_index = first_frame + 2 * jnp.arange(down_frames + 1, dtype=jnp.int32)
    mask_ext = tap_masks(positions(counts_row, down_index))
    down_mask = mask_ext[:down_frames]
    with_rows = padded_2(clips[0], (("height", 1),), 1)
    earlier = shifted(with_rows, "tm", 1)
    input_ext = jnp.concatenate([earlier, with_rows], axis=0)
    pre_act = conv_layer(input_ext, conv_first, first_mask, frames_dev, 1, (1, 1))
    hidden = jax.nn.silu(pre_act).astype(jnp.bfloat16)
    above = shifted(hidden[:, rows_dev - 1 :], "height", 1)
    hidden_rows = jnp.concatenate([above, hidden], axis=1)
    hidden_past = shifted(hidden_rows, "tm", 1)
    hidden_ext = jnp.concatenate([hidden_past, hidden_rows], axis=0)
    encoded = conv_layer(hidden_ext, conv_down, down_mask, down_frames, 2, (1, 0)).astype(
        jnp.bfloat16
    )
    cells_all = (
        lax.axis_size("dp")
        * clips.shape[0]
        * down_frames
        * lax.axis_size("tm")
        * (rows_dev // 2)
        * lax.axis_size("height")
        * (columns_all // 2)
    )
    scale = 1.0 / math.sqrt(cells_all)
    grads = (out_cotangent[0].astype(jnp.float32) * scale).astype(jnp.bfloat16)
    down_local = weight_grad(hidden_ext, grads, down_mask, 2, (1, 0))
    below = shifted(grads[:, 0:1], "height", -1)
    grads_rows = jnp.concatenate([grads, below], axis=1)
    grads_next = shifted(grads_rows, "tm", -1)
    grads_ext = jnp.concatenate([grads_rows, grads_next], axis=0)
    back_hidden = hidden_grad(grads_ext, conv_down, mask_ext).astype(jnp.bfloat16)
    sigma = jax.nn.sigmoid(pre_act)
    pre_grad = (back_hidden.astype(jnp.float32) * sigma * (1.0 + pre_act * (1.0 - sigma))).astype(
        jnp.bfloat16
    )
    first_local = weight_grad(input_ext, pre_grad, first_mask, 1, (1, 1))
    share = conv_first.shape[3] // lax.axis_size("dp")
    quarters = lax.axis_size("dp")

    def by_quarter(term):
        term = term.reshape(27, quarters, share, term.shape[-1])
        return jnp.transpose(term, (1, 0, 2, 3)).reshape(quarters, -1)

    stacked = jnp.concatenate([by_quarter(first_local), by_quarter(down_local)], axis=1)
    gathered = reduce_gradients(stacked).reshape(-1)
    half = gathered.shape[0] // 2
    kernel_shape = (3, 3, 3, share, conv_first.shape[-1])
    summed_first = gathered[:half].reshape(kernel_shape)
    summed_down = gathered[half:].reshape(kernel_shape)
    return (encoded[None], summed_first, summed_down)


def swap(value, axis, bit):
    return lax.ppermute(value, axis, [(i, i ^ bit) for i in range(lax.axis_size(axis))])


def bits_of(count):
    return [1 << k for k in range(count.bit_length() - 1)]


def split_bit(blocks, names, name, high):
    place = names.index(name)
    mine = lax.dynamic_index_in_dim(blocks, high, place, keepdims=False)
    other = lax.dynamic_index_in_dim(blocks, 1 - high, place, keepdims=False)
    return mine, other, names[:place] + names[place + 1 :]


def reduce_gradients(stacked):
    dp_bits = bits_of(lax.axis_size("dp"))
    row_bits = bits_of(lax.axis_size("height"))
    frame_bits = bits_of(lax.axis_size("tm"))
    names = [("dp", bit) for bit in reversed(dp_bits)] + [("height", bit) for bit in reversed(row_bits)]
    blocks = stacked.reshape((2,) * len(names) + (-1,))
    order = [("dp", bit) for bit in dp_bits[:-1]]
    near = row_bits[0::2] + row_bits[1::2]
    order += [("height", bit) for bit in near]
    for axis, bit in order:
        high = (lax.axis_index(axis) // bit) % 2
        mine, other, names = split_bit(blocks, names, (axis, bit), high)
        blocks = mine + swap(other, axis, bit)
    for bit in frame_bits:
        blocks = blocks + swap(blocks, "tm", bit)
    far = dp_bits[-1]
    high = (lax.axis_index("dp") // far) % 2
    mine, other, names = split_bit(blocks, names, ("dp", far), high)
    piece = (mine + swap(other, "dp", far)).astype(jnp.bfloat16)
    present = []
    for bit in reversed(near):
        other = swap(piece, "height", bit)
        high = (lax.axis_index("height") // bit) % 2
        place = sum(1 for held in present if held > bit)
        low_first = jnp.stack([piece, other], axis=place)
        high_first = jnp.stack([other, piece], axis=place)
        piece = jnp.where(high == 0, low_first, high_first)
        present.append(bit)
    return piece


def solution(mesh):
    in_specs = (
        P("dp", "tm", "height", None, None),
        P("dp", None),
        P(),
        P(),
        P("dp", "tm", "height", None, None),
    )
    out_specs = (
        P("dp", "tm", "height", None, None),
        P(None, None, None, "dp", None),
        P(None, None, None, "dp", None),
    )
    return jax.shard_map(body, mesh=mesh, in_specs=in_specs, out_specs=out_specs, check_vma=False)
```

```python
import math

import jax
import jax.numpy as jnp
from jax import lax
from jax.sharding import PartitionSpec as P


def padded_2(cells, sides, width):
    for axis, dim in sides:
        count = lax.axis_size(axis)
        ends = count - 1
        head = lax.slice_in_dim(cells, 0, width, axis=dim)
        tail = lax.slice_in_dim(cells, cells.shape[dim] - width, cells.shape[dim], axis=dim)
        cells = jnp.concatenate(
            [
                lax.ppermute(tail, axis, [(i, (i + 1) % count) for i in range(ends)]),
                cells,
                lax.ppermute(head, axis, [((i + 1) % count, i) for i in range(ends)]),
            ],
            axis=dim,
        )
    return cells


def shifted(value, axis, steps):
    count = lax.axis_size(axis)
    leading, last = (max(0, -steps), min(count, count - steps))
    return lax.ppermute(value, axis, [(source, source + steps) for source in range(leading, last)])


def unfold(frame_slab, stride, pad_cols):
    padded = jnp.pad(frame_slab, ((0, 0), (0, 0), pad_cols, (0, 0)))
    out_rows = (padded.shape[1] - 3) // stride + 1
    out_cols = (padded.shape[2] - 3) // stride + 1
    pieces = []
    for tap_row in range(3):
        for tap_col in range(3):
            pieces.append(
                padded[
                    :,
                    tap_row : tap_row + stride * (out_rows - 1) + 1 : stride,
                    tap_col : tap_col + stride * (out_cols - 1) + 1 : stride,
                ]
            )
    joined = jnp.concatenate(pieces, axis=-1)
    return (joined.reshape(-1, joined.shape[-1]), (frame_slab.shape[0], out_rows, out_cols))


def conv_layer(extended, weight, tap_mask, out_frames, stride, pad_cols):
    channels_out = weight.shape[-1]
    summed = None
    for tap_time in range(3):
        frame_slab = extended[tap_time : tap_time + stride * (out_frames - 1) + 1 : stride]
        columns, shape_out = unfold(frame_slab, stride, pad_cols)
        kernel = weight[tap_time].reshape(-1, channels_out)
        tap_term = jnp.dot(columns, kernel, preferred_element_type=jnp.float32).reshape(
            shape_out + (channels_out,)
        )
        tap_term = tap_term * tap_mask[:, tap_time][:, None, None, None]
        summed = tap_term if summed is None else summed + tap_term
    return summed


def weight_grad(extended, grads, tap_mask, stride, pad_cols):
    out_frames = grads.shape[0]
    blocks = []
    for tap_time in range(3):
        frame_slab = extended[tap_time : tap_time + stride * (out_frames - 1) + 1 : stride]
        columns, shape_out = unfold(frame_slab, stride, pad_cols)
        masked = grads * tap_mask[:, tap_time].astype(jnp.bfloat16)[:, None, None, None]
        blocks.append(
            jnp.dot(
                columns.T, masked.reshape(-1, grads.shape[-1]), preferred_element_type=jnp.float32
            )
        )
    stacked = jnp.stack(blocks)
    return stacked.reshape(3, 3, 3, extended.shape[-1], grads.shape[-1])


def hidden_grad(grads_ext, weight, mask_ext):
    pieces = []
    for tap_time in range(3):
        masked = grads_ext * mask_ext[:, tap_time].astype(jnp.bfloat16)[:, None, None, None]
        kernel = jnp.transpose(weight[tap_time][::-1, ::-1], (0, 1, 3, 2))
        spread = lax.conv_general_dilated(
            masked,
            kernel,
            (1, 1),
            ((2, 0), (2, 2)),
            lhs_dilation=(2, 2),
            dimension_numbers=("NHWC", "HWIO", "NHWC"),
            preferred_element_type=jnp.float32,
        )
        pieces.append(spread[:, 1:, 1:])
    even_frames = pieces[2][:-1] + pieces[0][1:]
    odd_frames = pieces[1][1:]
    merged = jnp.stack([even_frames, odd_frames], axis=1)
    return merged.reshape((2 * even_frames.shape[0],) + even_frames.shape[1:])


def positions(counts_row, frame_index):
    starts = jnp.cumsum(counts_row) - counts_row
    latest = jnp.max(jnp.where(starts[None, :] <= frame_index[:, None], starts[None, :], 0), axis=1)
    return frame_index - latest


def tap_masks(place):
    return (place[:, None] >= (2 - jnp.arange(3, dtype=jnp.int32))[None, :]).astype(jnp.float32)


def body(clips, frame_counts, conv_first, conv_down, out_cotangent):
    frames_dev = clips.shape[1]
    rows_dev = clips.shape[2]
    columns_all = clips.shape[3]
    down_frames = frames_dev // 2
    counts_row = frame_counts[0]
    first_frame = lax.axis_index("tm") * frames_dev
    frame_index = first_frame + jnp.arange(frames_dev, dtype=jnp.int32)
    first_mask = tap_masks(positions(counts_row, frame_index))
    down_index = first_frame + 2 * jnp.arange(down_frames + 1, dtype=jnp.int32)
    mask_ext = tap_masks(positions(counts_row, down_index))
    down_mask = mask_ext[:down_frames]
    with_rows = padded_2(clips[0], (("height", 1),), 1)
    earlier = shifted(with_rows, "tm", 1)
    input_ext = jnp.concatenate([earlier, with_rows], axis=0)
    pre_act = conv_layer(input_ext, conv_first, first_mask, frames_dev, 1, (1, 1))
    hidden = jax.nn.silu(pre_act).astype(jnp.bfloat16)
    above = shifted(hidden[:, rows_dev - 1 :], "height", 1)
    hidden_rows = jnp.concatenate([above, hidden], axis=1)
    hidden_past = shifted(hidden_rows, "tm", 1)
    hidden_ext = jnp.concatenate([hidden_past, hidden_rows], axis=0)
    encoded = conv_layer(hidden_ext, conv_down, down_mask, down_frames, 2, (1, 0)).astype(
        jnp.bfloat16
    )
    cells_all = (
        lax.axis_size("dp")
        * clips.shape[0]
        * down_frames
        * lax.axis_size("tm")
        * (rows_dev // 2)
        * lax.axis_size("height")
        * (columns_all // 2)
    )
    scale = 1.0 / math.sqrt(cells_all)
    grads = (out_cotangent[0].astype(jnp.float32) * scale).astype(jnp.bfloat16)
    down_local = weight_grad(hidden_ext, grads, down_mask, 2, (1, 0))
    below = shifted(grads[:, 0:1], "height", -1)
    grads_rows = jnp.concatenate([grads, below], axis=1)
    grads_next = shifted(grads_rows, "tm", -1)
    grads_ext = jnp.concatenate([grads_rows, grads_next], axis=0)
    back_hidden = hidden_grad(grads_ext, conv_down, mask_ext).astype(jnp.bfloat16)
    sigma = jax.nn.sigmoid(pre_act)
    pre_grad = (back_hidden.astype(jnp.float32) * sigma * (1.0 + pre_act * (1.0 - sigma))).astype(
        jnp.bfloat16
    )
    first_local = weight_grad(input_ext, pre_grad, first_mask, 1, (1, 1))
    share = conv_first.shape[3] // lax.axis_size("dp")
    quarters = lax.axis_size("dp")

    def by_quarter(term):
        term = term.reshape(27, quarters, share, term.shape[-1])
        return jnp.transpose(term, (1, 0, 2, 3)).reshape(quarters, -1)

    stacked = jnp.concatenate([by_quarter(first_local), by_quarter(down_local)], axis=1)
    gathered = reduce_gradients(stacked).reshape(-1)
    half = gathered.shape[0] // 2
    kernel_shape = (3, 3, 3, share, conv_first.shape[-1])
    summed_first = gathered[:half].reshape(kernel_shape)
    summed_down = gathered[half:].reshape(kernel_shape)
    return (encoded[None], summed_first, summed_down)


def swap(value, axis, bit):
    return lax.ppermute(value, axis, [(i, i ^ bit) for i in range(lax.axis_size(axis))])


def swap_rows(value, bits):
    count = lax.axis_size("height")
    pairs = []
    for group in range(lax.axis_size("dp")):
        bit = bits[group % 2]
        pairs += [(group * count + i, group * count + (i ^ bit)) for i in range(count)]
    return lax.ppermute(value, ("dp", "height"), pairs)


def bits_of(count):
    return [1 << k for k in range(count.bit_length() - 1)]


def split_bit(blocks, names, name, high):
    place = names.index(name)
    mine = lax.dynamic_index_in_dim(blocks, high, place, keepdims=False)
    other = lax.dynamic_index_in_dim(blocks, 1 - high, place, keepdims=False)
    return mine, other, names[:place] + names[place + 1 :]


def reduce_gradients(stacked):
    dp_bits = bits_of(lax.axis_size("dp"))
    row_bits = bits_of(lax.axis_size("height"))
    frame_bits = bits_of(lax.axis_size("tm"))
    names = [("dp", bit) for bit in reversed(dp_bits)] + [("height", bit) for bit in reversed(row_bits)]
    blocks = stacked.reshape((2,) * len(names) + (-1,))
    for bit in dp_bits[:-1]:
        high = (lax.axis_index("dp") // bit) % 2
        mine, other, names = split_bit(blocks, names, ("dp", bit), high)
        blocks = mine + swap(other, "dp", bit)
    near = row_bits[0::2] + row_bits[1::2]
    crossed = [near[k ^ 1] if (k ^ 1) < len(near) else near[k] for k in range(len(near))]
    stages = list(zip(near, crossed))
    core = lax.axis_index("dp") % 2
    row = lax.axis_index("height")
    held = [names, names]
    for bits in stages:
        parts = []
        for variant in (0, 1):
            high = (row // bits[variant]) % 2
            mine, other, held[variant] = split_bit(blocks, held[variant], ("height", bits[variant]), high)
            parts.append((mine, other))
        mine = jnp.where(core == 0, parts[0][0], parts[1][0])
        other = jnp.where(core == 0, parts[0][1], parts[1][1])
        blocks = mine + swap_rows(other, bits)
    far = dp_bits[-1]
    high = (lax.axis_index("dp") // far) % 2
    mine, other, _ = split_bit(blocks, held[0], ("dp", far), high)
    blocks = mine + swap(other, "dp", far)
    for bit in frame_bits:
        blocks = blocks + swap(blocks, "tm", bit)
    piece = blocks.astype(jnp.bfloat16)
    present = [[], []]
    for bits in reversed(stages):
        other = swap_rows(piece, bits)
        options = []
        for variant in (0, 1):
            bit = bits[variant]
            high = (row // bit) % 2
            place = sum(1 for kept in present[variant] if kept > bit)
            low_first = jnp.stack([piece, other], axis=place)
            high_first = jnp.stack([other, piece], axis=place)
            options.append(jnp.where(high == 0, low_first, high_first))
            present[variant].append(bit)
        piece = jnp.where(core == 0, options[0], options[1])
    return piece


def solution(mesh):
    in_specs = (
        P("dp", "tm", "height", None, None),
        P("dp", None),
        P(),
        P(),
        P("dp", "tm", "height", None, None),
    )
    out_specs = (
        P("dp", "tm", "height", None, None),
        P(None, None, None, "dp", None),
        P(None, None, None, "dp", None),
    )
    return jax.shard_map(body, mesh=mesh, in_specs=in_specs, out_specs=out_specs, check_vma=False)
```

```python
import math

import jax
import jax.numpy as jnp
from jax import lax
from jax.sharding import PartitionSpec as P


def padded_2(cells, sides, width):
    for axis, dim in sides:
        count = lax.axis_size(axis)
        ends = count - 1
        head = lax.slice_in_dim(cells, 0, width, axis=dim)
        tail = lax.slice_in_dim(cells, cells.shape[dim] - width, cells.shape[dim], axis=dim)
        cells = jnp.concatenate(
            [
                lax.ppermute(tail, axis, [(i, (i + 1) % count) for i in range(ends)]),
                cells,
                lax.ppermute(head, axis, [((i + 1) % count, i) for i in range(ends)]),
            ],
            axis=dim,
        )
    return cells


def shifted(value, axis, steps):
    count = lax.axis_size(axis)
    leading, last = (max(0, -steps), min(count, count - steps))
    return lax.ppermute(value, axis, [(source, source + steps) for source in range(leading, last)])


def unfold(frame_slab, stride, pad_cols):
    padded = jnp.pad(frame_slab, ((0, 0), (0, 0), pad_cols, (0, 0)))
    out_rows = (padded.shape[1] - 3) // stride + 1
    out_cols = (padded.shape[2] - 3) // stride + 1
    pieces = []
    for tap_row in range(3):
        for tap_col in range(3):
            pieces.append(
                padded[
                    :,
                    tap_row : tap_row + stride * (out_rows - 1) + 1 : stride,
                    tap_col : tap_col + stride * (out_cols - 1) + 1 : stride,
                ]
            )
    joined = jnp.concatenate(pieces, axis=-1)
    return (joined.reshape(-1, joined.shape[-1]), (frame_slab.shape[0], out_rows, out_cols))


def conv_layer(extended, weight, tap_mask, out_frames, stride, pad_cols):
    channels_out = weight.shape[-1]
    summed = None
    for tap_time in range(3):
        frame_slab = extended[tap_time : tap_time + stride * (out_frames - 1) + 1 : stride]
        columns, shape_out = unfold(frame_slab, stride, pad_cols)
        kernel = weight[tap_time].reshape(-1, channels_out)
        tap_term = jnp.dot(columns, kernel, preferred_element_type=jnp.float32).reshape(
            shape_out + (channels_out,)
        )
        tap_term = tap_term * tap_mask[:, tap_time][:, None, None, None]
        summed = tap_term if summed is None else summed + tap_term
    return summed


def weight_grad(extended, grads, tap_mask, stride, pad_cols):
    out_frames = grads.shape[0]
    blocks = []
    for tap_time in range(3):
        frame_slab = extended[tap_time : tap_time + stride * (out_frames - 1) + 1 : stride]
        columns, shape_out = unfold(frame_slab, stride, pad_cols)
        masked = grads * tap_mask[:, tap_time].astype(jnp.bfloat16)[:, None, None, None]
        blocks.append(
            jnp.dot(
                columns.T, masked.reshape(-1, grads.shape[-1]), preferred_element_type=jnp.float32
            )
        )
    stacked = jnp.stack(blocks)
    return stacked.reshape(3, 3, 3, extended.shape[-1], grads.shape[-1])


def hidden_grad(grads_ext, weight, mask_ext):
    pieces = []
    for tap_time in range(3):
        masked = grads_ext * mask_ext[:, tap_time].astype(jnp.bfloat16)[:, None, None, None]
        kernel = jnp.transpose(weight[tap_time][::-1, ::-1], (0, 1, 3, 2))
        spread = lax.conv_general_dilated(
            masked,
            kernel,
            (1, 1),
            ((2, 0), (2, 2)),
            lhs_dilation=(2, 2),
            dimension_numbers=("NHWC", "HWIO", "NHWC"),
            preferred_element_type=jnp.float32,
        )
        pieces.append(spread[:, 1:, 1:])
    even_frames = pieces[2][:-1] + pieces[0][1:]
    odd_frames = pieces[1][1:]
    merged = jnp.stack([even_frames, odd_frames], axis=1)
    return merged.reshape((2 * even_frames.shape[0],) + even_frames.shape[1:])


def positions(counts_row, frame_index):
    starts = jnp.cumsum(counts_row) - counts_row
    latest = jnp.max(jnp.where(starts[None, :] <= frame_index[:, None], starts[None, :], 0), axis=1)
    return frame_index - latest


def tap_masks(place):
    return (place[:, None] >= (2 - jnp.arange(3, dtype=jnp.int32))[None, :]).astype(jnp.float32)


def body(clips, frame_counts, conv_first, conv_down, out_cotangent):
    frames_dev = clips.shape[1]
    rows_dev = clips.shape[2]
    columns_all = clips.shape[3]
    down_frames = frames_dev // 2
    counts_row = frame_counts[0]
    first_frame = lax.axis_index("tm") * frames_dev
    frame_index = first_frame + jnp.arange(frames_dev, dtype=jnp.int32)
    first_mask = tap_masks(positions(counts_row, frame_index))
    down_index = first_frame + 2 * jnp.arange(down_frames + 1, dtype=jnp.int32)
    mask_ext = tap_masks(positions(counts_row, down_index))
    down_mask = mask_ext[:down_frames]
    with_rows = padded_2(clips[0], (("height", 1),), 1)
    earlier = shifted(with_rows, "tm", 1)
    input_ext = jnp.concatenate([earlier, with_rows], axis=0)
    pre_act = conv_layer(input_ext, conv_first, first_mask, frames_dev, 1, (1, 1))
    hidden = jax.nn.silu(pre_act).astype(jnp.bfloat16)
    above = shifted(hidden[:, rows_dev - 1 :], "height", 1)
    hidden_rows = jnp.concatenate([above, hidden], axis=1)
    hidden_past = shifted(hidden_rows, "tm", 1)
    hidden_ext = jnp.concatenate([hidden_past, hidden_rows], axis=0)
    encoded = conv_layer(hidden_ext, conv_down, down_mask, down_frames, 2, (1, 0)).astype(
        jnp.bfloat16
    )
    cells_all = (
        lax.axis_size("dp")
        * clips.shape[0]
        * down_frames
        * lax.axis_size("tm")
        * (rows_dev // 2)
        * lax.axis_size("height")
        * (columns_all // 2)
    )
    scale = 1.0 / math.sqrt(cells_all)
    grads = (out_cotangent[0].astype(jnp.float32) * scale).astype(jnp.bfloat16)
    down_local = weight_grad(hidden_ext, grads, down_mask, 2, (1, 0))
    below = shifted(grads[:, 0:1], "height", -1)
    grads_rows = jnp.concatenate([grads, below], axis=1)
    grads_next = shifted(grads_rows, "tm", -1)
    grads_ext = jnp.concatenate([grads_rows, grads_next], axis=0)
    back_hidden = hidden_grad(grads_ext, conv_down, mask_ext).astype(jnp.bfloat16)
    sigma = jax.nn.sigmoid(pre_act)
    pre_grad = (back_hidden.astype(jnp.float32) * sigma * (1.0 + pre_act * (1.0 - sigma))).astype(
        jnp.bfloat16
    )
    first_local = weight_grad(input_ext, pre_grad, first_mask, 1, (1, 1))
    share = conv_first.shape[3] // lax.axis_size("dp")
    quarters = lax.axis_size("dp")

    def by_quarter(term):
        term = term.reshape(27, quarters, share, term.shape[-1])
        return jnp.transpose(term, (1, 0, 2, 3)).reshape(quarters, -1)

    stacked = jnp.concatenate([by_quarter(first_local), by_quarter(down_local)], axis=1)
    gathered = reduce_gradients(stacked).reshape(-1)
    half = gathered.shape[0] // 2
    kernel_shape = (3, 3, 3, share, conv_first.shape[-1])
    summed_first = gathered[:half].reshape(kernel_shape)
    summed_down = gathered[half:].reshape(kernel_shape)
    return (encoded[None], summed_first, summed_down)


def swap(value, axis, bit):
    return lax.ppermute(value, axis, [(i, i ^ bit) for i in range(lax.axis_size(axis))])


def swap_rows(value, bits):
    count = lax.axis_size("height")
    pairs = []
    for group in range(lax.axis_size("dp")):
        bit = bits[group % 2]
        pairs += [(group * count + i, group * count + (i ^ bit)) for i in range(count)]
    return lax.ppermute(value, ("dp", "height"), pairs)


def bits_of(count):
    return [1 << k for k in range(count.bit_length() - 1)]


def split_bit(blocks, names, name, high):
    place = names.index(name)
    mine = lax.dynamic_index_in_dim(blocks, high, place, keepdims=False)
    other = lax.dynamic_index_in_dim(blocks, 1 - high, place, keepdims=False)
    return mine, other, names[:place] + names[place + 1 :]


def reduce_gradients(stacked):
    dp_bits = bits_of(lax.axis_size("dp"))
    row_bits = bits_of(lax.axis_size("height"))
    frame_bits = bits_of(lax.axis_size("tm"))
    names = [("dp", bit) for bit in reversed(dp_bits)] + [("height", bit) for bit in reversed(row_bits)]
    blocks = stacked.reshape((2,) * len(names) + (-1, 128))
    for bit in dp_bits[:-1]:
        high = (lax.axis_index("dp") // bit) % 2
        mine, other, names = split_bit(blocks, names, ("dp", bit), high)
        blocks = mine + swap(other, "dp", bit)
    near = row_bits[0::2] + row_bits[1::2]
    crossed = [near[k ^ 1] if (k ^ 1) < len(near) else near[k] for k in range(len(near))]
    stages = list(zip(near, crossed))
    core = lax.axis_index("dp") % 2
    row = lax.axis_index("height")
    held = [names, names]
    for bits in stages:
        parts = []
        for variant in (0, 1):
            high = (row // bits[variant]) % 2
            mine, other, held[variant] = split_bit(blocks, held[variant], ("height", bits[variant]), high)
            parts.append((mine, other))
        mine = jnp.where(core == 0, parts[0][0], parts[1][0])
        other = jnp.where(core == 0, parts[0][1], parts[1][1])
        blocks = mine + swap_rows(other, bits)
    far = dp_bits[-1]
    high = (lax.axis_index("dp") // far) % 2
    mine, other, _ = split_bit(blocks, held[0], ("dp", far), high)
    blocks = mine + swap(other, "dp", far)
    for bit in frame_bits:
        blocks = blocks + swap(blocks, "tm", bit)
    piece = blocks.astype(jnp.bfloat16)
    present = [[], []]
    for bits in reversed(stages):
        other = swap_rows(piece, bits)
        options = []
        for variant in (0, 1):
            bit = bits[variant]
            high = (row // bit) % 2
            place = sum(1 for kept in present[variant] if kept > bit)
            low_first = jnp.stack([piece, other], axis=place)
            high_first = jnp.stack([other, piece], axis=place)
            options.append(jnp.where(high == 0, low_first, high_first))
            present[variant].append(bit)
        piece = jnp.where(core == 0, options[0], options[1])
    return piece


def solution(mesh):
    in_specs = (
        P("dp", "tm", "height", None, None),
        P("dp", None),
        P(),
        P(),
        P("dp", "tm", "height", None, None),
    )
    out_specs = (
        P("dp", "tm", "height", None, None),
        P(None, None, None, "dp", None),
        P(None, None, None, "dp", None),
    )
    return jax.shard_map(body, mesh=mesh, in_specs=in_specs, out_specs=out_specs, check_vma=False)
```

```python
import math

import jax
import jax.numpy as jnp
from jax import lax
from jax.sharding import PartitionSpec as P


def padded_2(cells, sides, width):
    for axis, dim in sides:
        count = lax.axis_size(axis)
        ends = count - 1
        head = lax.slice_in_dim(cells, 0, width, axis=dim)
        tail = lax.slice_in_dim(cells, cells.shape[dim] - width, cells.shape[dim], axis=dim)
        cells = jnp.concatenate(
            [
                lax.ppermute(tail, axis, [(i, (i + 1) % count) for i in range(ends)]),
                cells,
                lax.ppermute(head, axis, [((i + 1) % count, i) for i in range(ends)]),
            ],
            axis=dim,
        )
    return cells


def shifted(value, axis, steps):
    count = lax.axis_size(axis)
    leading, last = (max(0, -steps), min(count, count - steps))
    return lax.ppermute(value, axis, [(source, source + steps) for source in range(leading, last)])


def unfold(frame_slab, stride, pad_cols):
    padded = jnp.pad(frame_slab, ((0, 0), (0, 0), pad_cols, (0, 0)))
    out_rows = (padded.shape[1] - 3) // stride + 1
    out_cols = (padded.shape[2] - 3) // stride + 1
    pieces = []
    for tap_row in range(3):
        for tap_col in range(3):
            pieces.append(
                padded[
                    :,
                    tap_row : tap_row + stride * (out_rows - 1) + 1 : stride,
                    tap_col : tap_col + stride * (out_cols - 1) + 1 : stride,
                ]
            )
    joined = jnp.concatenate(pieces, axis=-1)
    return (joined.reshape(-1, joined.shape[-1]), (frame_slab.shape[0], out_rows, out_cols))


def conv_layer(extended, weight, tap_mask, out_frames, stride, pad_cols):
    channels_out = weight.shape[-1]
    summed = None
    for tap_time in range(3):
        frame_slab = extended[tap_time : tap_time + stride * (out_frames - 1) + 1 : stride]
        columns, shape_out = unfold(frame_slab, stride, pad_cols)
        kernel = weight[tap_time].reshape(-1, channels_out)
        tap_term = jnp.dot(columns, kernel, preferred_element_type=jnp.float32).reshape(
            shape_out + (channels_out,)
        )
        tap_term = tap_term * tap_mask[:, tap_time][:, None, None, None]
        summed = tap_term if summed is None else summed + tap_term
    return summed


def weight_grad(extended, grads, tap_mask, stride, pad_cols):
    out_frames = grads.shape[0]
    blocks = []
    for tap_time in range(3):
        frame_slab = extended[tap_time : tap_time + stride * (out_frames - 1) + 1 : stride]
        columns, shape_out = unfold(frame_slab, stride, pad_cols)
        masked = grads * tap_mask[:, tap_time].astype(jnp.bfloat16)[:, None, None, None]
        blocks.append(
            jnp.dot(
                columns.T, masked.reshape(-1, grads.shape[-1]), preferred_element_type=jnp.float32
            )
        )
    stacked = jnp.stack(blocks)
    return stacked.reshape(3, 3, 3, extended.shape[-1], grads.shape[-1])


def hidden_grad(grads_ext, weight, mask_ext):
    pieces = []
    for tap_time in range(3):
        masked = grads_ext * mask_ext[:, tap_time].astype(jnp.bfloat16)[:, None, None, None]
        kernel = jnp.transpose(weight[tap_time][::-1, ::-1], (0, 1, 3, 2))
        spread = lax.conv_general_dilated(
            masked,
            kernel,
            (1, 1),
            ((2, 0), (2, 2)),
            lhs_dilation=(2, 2),
            dimension_numbers=("NHWC", "HWIO", "NHWC"),
            preferred_element_type=jnp.float32,
        )
        pieces.append(spread[:, 1:, 1:])
    even_frames = pieces[2][:-1] + pieces[0][1:]
    odd_frames = pieces[1][1:]
    merged = jnp.stack([even_frames, odd_frames], axis=1)
    return merged.reshape((2 * even_frames.shape[0],) + even_frames.shape[1:])


def positions(counts_row, frame_index):
    starts = jnp.cumsum(counts_row) - counts_row
    latest = jnp.max(jnp.where(starts[None, :] <= frame_index[:, None], starts[None, :], 0), axis=1)
    return frame_index - latest


def tap_masks(place):
    return (place[:, None] >= (2 - jnp.arange(3, dtype=jnp.int32))[None, :]).astype(jnp.float32)


def body(clips, frame_counts, conv_first, conv_down, out_cotangent):
    frames_dev = clips.shape[1]
    rows_dev = clips.shape[2]
    columns_all = clips.shape[3]
    down_frames = frames_dev // 2
    counts_row = frame_counts[0]
    first_frame = lax.axis_index("tm") * frames_dev
    frame_index = first_frame + jnp.arange(frames_dev, dtype=jnp.int32)
    first_mask = tap_masks(positions(counts_row, frame_index))
    down_index = first_frame + 2 * jnp.arange(down_frames + 1, dtype=jnp.int32)
    mask_ext = tap_masks(positions(counts_row, down_index))
    down_mask = mask_ext[:down_frames]
    with_rows = padded_2(clips[0], (("height", 1),), 1)
    earlier = shifted(with_rows, "tm", 1)
    input_ext = jnp.concatenate([earlier, with_rows], axis=0)
    pre_act = conv_layer(input_ext, conv_first, first_mask, frames_dev, 1, (1, 1))
    hidden = jax.nn.silu(pre_act).astype(jnp.bfloat16)
    above = shifted(hidden[:, rows_dev - 1 :], "height", 1)
    hidden_rows = jnp.concatenate([above, hidden], axis=1)
    hidden_past = shifted(hidden_rows, "tm", 1)
    hidden_ext = jnp.concatenate([hidden_past, hidden_rows], axis=0)
    encoded = conv_layer(hidden_ext, conv_down, down_mask, down_frames, 2, (1, 0)).astype(
        jnp.bfloat16
    )
    cells_all = (
        lax.axis_size("dp")
        * clips.shape[0]
        * down_frames
        * lax.axis_size("tm")
        * (rows_dev // 2)
        * lax.axis_size("height")
        * (columns_all // 2)
    )
    scale = 1.0 / math.sqrt(cells_all)
    grads = (out_cotangent[0].astype(jnp.float32) * scale).astype(jnp.bfloat16)
    down_local = weight_grad(hidden_ext, grads, down_mask, 2, (1, 0))
    below = shifted(grads[:, 0:1], "height", -1)
    grads_rows = jnp.concatenate([grads, below], axis=1)
    grads_next = shifted(grads_rows, "tm", -1)
    grads_ext = jnp.concatenate([grads_rows, grads_next], axis=0)
    back_hidden = hidden_grad(grads_ext, conv_down, mask_ext).astype(jnp.bfloat16)
    sigma = jax.nn.sigmoid(pre_act)
    pre_grad = (back_hidden.astype(jnp.float32) * sigma * (1.0 + pre_act * (1.0 - sigma))).astype(
        jnp.bfloat16
    )
    first_local = weight_grad(input_ext, pre_grad, first_mask, 1, (1, 1))
    share = conv_first.shape[3] // lax.axis_size("dp")
    quarters = lax.axis_size("dp")

    lanes = conv_first.shape[-1]
    rows_total = 27 * share
    chunks = lax.axis_size("height") // 2
    chunk_rows = -(-rows_total // (chunks * 16)) * 16
    padded_rows = chunk_rows * chunks

    def by_quarter(term):
        term = term.reshape(27, quarters, share, lanes)
        term = jnp.transpose(term, (1, 0, 2, 3)).reshape(quarters, rows_total, lanes)
        return jnp.pad(term, ((0, 0), (0, padded_rows - rows_total), (0, 0)))

    stacked = jnp.stack([by_quarter(first_local), by_quarter(down_local)], axis=1)
    gathered = reduce_gradients(stacked).reshape(2, padded_rows, lanes)[:, :rows_total]
    kernel_shape = (3, 3, 3, share, lanes)
    summed_first = gathered[0].reshape(kernel_shape)
    summed_down = gathered[1].reshape(kernel_shape)
    return (encoded[None], summed_first, summed_down)


def swap(value, axis, bit):
    return lax.ppermute(value, axis, [(i, i ^ bit) for i in range(lax.axis_size(axis))])


def swap_rows(value, bits):
    count = lax.axis_size("height")
    pairs = []
    for group in range(lax.axis_size("dp")):
        bit = bits[group % 2]
        pairs += [(group * count + i, group * count + (i ^ bit)) for i in range(count)]
    return lax.ppermute(value, ("dp", "height"), pairs)


def bits_of(count):
    return [1 << k for k in range(count.bit_length() - 1)]


def split_bit(blocks, names, name, high):
    place = names.index(name)
    mine = lax.dynamic_index_in_dim(blocks, high, place, keepdims=False)
    other = lax.dynamic_index_in_dim(blocks, 1 - high, place, keepdims=False)
    return mine, other, names[:place] + names[place + 1 :]


def reduce_gradients(stacked):
    dp_bits = bits_of(lax.axis_size("dp"))
    row_bits = bits_of(lax.axis_size("height"))
    frame_bits = bits_of(lax.axis_size("tm"))
    names = [("dp", bit) for bit in reversed(dp_bits)] + [("height", bit) for bit in reversed(row_bits)]
    blocks = stacked.reshape((2,) * len(names) + (-1, 128))
    for bit in dp_bits[:-1]:
        high = (lax.axis_index("dp") // bit) % 2
        mine, other, names = split_bit(blocks, names, ("dp", bit), high)
        blocks = mine + swap(other, "dp", bit)
    near = row_bits[0::2] + row_bits[1::2]
    crossed = [near[k ^ 1] if (k ^ 1) < len(near) else near[k] for k in range(len(near))]
    stages = list(zip(near, crossed))
    core = lax.axis_index("dp") % 2
    row = lax.axis_index("height")
    held = [names, names]
    for bits in stages:
        parts = []
        for variant in (0, 1):
            high = (row // bits[variant]) % 2
            mine, other, held[variant] = split_bit(blocks, held[variant], ("height", bits[variant]), high)
            parts.append((mine, other))
        mine = jnp.where(core == 0, parts[0][0], parts[1][0])
        other = jnp.where(core == 0, parts[0][1], parts[1][1])
        blocks = mine + swap_rows(other, bits)
    far = dp_bits[-1]
    high = (lax.axis_index("dp") // far) % 2
    mine, other, _ = split_bit(blocks, held[0], ("dp", far), high)
    blocks = mine + swap(other, "dp", far)
    for bit in frame_bits:
        blocks = blocks + swap(blocks, "tm", bit)
    piece = blocks.astype(jnp.bfloat16)
    present = [[], []]
    for bits in reversed(stages):
        other = swap_rows(piece, bits)
        options = []
        for variant in (0, 1):
            bit = bits[variant]
            high = (row // bit) % 2
            place = sum(1 for kept in present[variant] if kept > bit)
            low_first = jnp.stack([piece, other], axis=place)
            high_first = jnp.stack([other, piece], axis=place)
            options.append(jnp.where(high == 0, low_first, high_first))
            present[variant].append(bit)
        piece = jnp.where(core == 0, options[0], options[1])
    return piece


def solution(mesh):
    in_specs = (
        P("dp", "tm", "height", None, None),
        P("dp", None),
        P(),
        P(),
        P("dp", "tm", "height", None, None),
    )
    out_specs = (
        P("dp", "tm", "height", None, None),
        P(None, None, None, "dp", None),
        P(None, None, None, "dp", None),
    )
    return jax.shard_map(body, mesh=mesh, in_specs=in_specs, out_specs=out_specs, check_vma=False)
```

```python
import math

import jax
import jax.numpy as jnp
from jax import lax
from jax.sharding import PartitionSpec as P


def padded_2(cells, sides, width):
    for axis, dim in sides:
        count = lax.axis_size(axis)
        ends = count - 1
        head = lax.slice_in_dim(cells, 0, width, axis=dim)
        tail = lax.slice_in_dim(cells, cells.shape[dim] - width, cells.shape[dim], axis=dim)
        cells = jnp.concatenate(
            [
                lax.ppermute(tail, axis, [(i, (i + 1) % count) for i in range(ends)]),
                cells,
                lax.ppermute(head, axis, [((i + 1) % count, i) for i in range(ends)]),
            ],
            axis=dim,
        )
    return cells


def shifted(value, axis, steps):
    count = lax.axis_size(axis)
    leading, last = (max(0, -steps), min(count, count - steps))
    return lax.ppermute(value, axis, [(source, source + steps) for source in range(leading, last)])


def conv_layer(extended, weight, tap_mask, out_frames, stride, pad_cols):
    summed = None
    for tap_time in range(3):
        frame_slab = extended[tap_time : tap_time + stride * (out_frames - 1) + 1 : stride]
        tap_term = lax.conv_general_dilated(
            frame_slab,
            weight[tap_time],
            (stride, stride),
            ((0, 0), pad_cols),
            dimension_numbers=("NHWC", "HWIO", "NHWC"),
            preferred_element_type=jnp.float32,
        )
        tap_term = tap_term * tap_mask[:, tap_time][:, None, None, None]
        summed = tap_term if summed is None else summed + tap_term
    return summed


def weight_grad(extended, grads, tap_mask, stride, pad_cols):
    out_frames = grads.shape[0]
    blocks = []
    for tap_time in range(3):
        frame_slab = extended[tap_time : tap_time + stride * (out_frames - 1) + 1 : stride]
        masked = grads * tap_mask[:, tap_time].astype(jnp.bfloat16)[:, None, None, None]
        blocks.append(
            lax.conv_general_dilated(
                frame_slab,
                masked,
                (1, 1),
                ((0, 0), pad_cols),
                rhs_dilation=(stride, stride),
                dimension_numbers=("CHWN", "IHWO", "HWNC"),
                preferred_element_type=jnp.float32,
            )
        )
    return jnp.stack(blocks)


def hidden_grad(grads_ext, weight, mask_ext):
    pieces = []
    for tap_time in range(3):
        masked = grads_ext * mask_ext[:, tap_time].astype(jnp.bfloat16)[:, None, None, None]
        kernel = jnp.transpose(weight[tap_time][::-1, ::-1], (0, 1, 3, 2))
        spread = lax.conv_general_dilated(
            masked,
            kernel,
            (1, 1),
            ((2, 0), (2, 2)),
            lhs_dilation=(2, 2),
            dimension_numbers=("NHWC", "HWIO", "NHWC"),
            preferred_element_type=jnp.float32,
        )
        pieces.append(spread[:, 1:, 1:])
    even_frames = pieces[2][:-1] + pieces[0][1:]
    odd_frames = pieces[1][1:]
    merged = jnp.stack([even_frames, odd_frames], axis=1)
    return merged.reshape((2 * even_frames.shape[0],) + even_frames.shape[1:])


def positions(counts_row, frame_index):
    starts = jnp.cumsum(counts_row) - counts_row
    latest = jnp.max(jnp.where(starts[None, :] <= frame_index[:, None], starts[None, :], 0), axis=1)
    return frame_index - latest


def tap_masks(place):
    return (place[:, None] >= (2 - jnp.arange(3, dtype=jnp.int32))[None, :]).astype(jnp.float32)


def body(clips, frame_counts, conv_first, conv_down, out_cotangent):
    frames_dev = clips.shape[1]
    rows_dev = clips.shape[2]
    columns_all = clips.shape[3]
    down_frames = frames_dev // 2
    counts_row = frame_counts[0]
    first_frame = lax.axis_index("tm") * frames_dev
    frame_index = first_frame + jnp.arange(frames_dev, dtype=jnp.int32)
    first_mask = tap_masks(positions(counts_row, frame_index))
    down_index = first_frame + 2 * jnp.arange(down_frames + 1, dtype=jnp.int32)
    mask_ext = tap_masks(positions(counts_row, down_index))
    down_mask = mask_ext[:down_frames]
    with_rows = padded_2(clips[0], (("height", 1),), 1)
    earlier = shifted(with_rows, "tm", 1)
    input_ext = jnp.concatenate([earlier, with_rows], axis=0)
    pre_act = conv_layer(input_ext, conv_first, first_mask, frames_dev, 1, (1, 1))
    hidden = jax.nn.silu(pre_act).astype(jnp.bfloat16)
    above = shifted(hidden[:, rows_dev - 1 :], "height", 1)
    hidden_rows = jnp.concatenate([above, hidden], axis=1)
    hidden_past = shifted(hidden_rows, "tm", 1)
    hidden_ext = jnp.concatenate([hidden_past, hidden_rows], axis=0)
    encoded = conv_layer(hidden_ext, conv_down, down_mask, down_frames, 2, (1, 0)).astype(
        jnp.bfloat16
    )
    cells_all = (
        lax.axis_size("dp")
        * clips.shape[0]
        * down_frames
        * lax.axis_size("tm")
        * (rows_dev // 2)
        * lax.axis_size("height")
        * (columns_all // 2)
    )
    scale = 1.0 / math.sqrt(cells_all)
    grads = (out_cotangent[0].astype(jnp.float32) * scale).astype(jnp.bfloat16)
    down_local = weight_grad(hidden_ext, grads, down_mask, 2, (1, 0))
    below = shifted(grads[:, 0:1], "height", -1)
    grads_rows = jnp.concatenate([grads, below], axis=1)
    grads_next = shifted(grads_rows, "tm", -1)
    grads_ext = jnp.concatenate([grads_rows, grads_next], axis=0)
    back_hidden = hidden_grad(grads_ext, conv_down, mask_ext).astype(jnp.bfloat16)
    sigma = jax.nn.sigmoid(pre_act)
    pre_grad = (back_hidden.astype(jnp.float32) * sigma * (1.0 + pre_act * (1.0 - sigma))).astype(
        jnp.bfloat16
    )
    first_local = weight_grad(input_ext, pre_grad, first_mask, 1, (1, 1))
    share = conv_first.shape[3] // lax.axis_size("dp")
    quarters = lax.axis_size("dp")

    lanes = conv_first.shape[-1]
    rows_total = 27 * share
    chunks = lax.axis_size("height") // 2
    chunk_rows = -(-rows_total // (chunks * 16)) * 16
    padded_rows = chunk_rows * chunks

    def by_quarter(term):
        term = term.reshape(27, quarters, share, lanes)
        term = jnp.transpose(term, (1, 0, 2, 3)).reshape(quarters, rows_total, lanes)
        return jnp.pad(term, ((0, 0), (0, padded_rows - rows_total), (0, 0)))

    stacked = jnp.stack([by_quarter(first_local), by_quarter(down_local)], axis=1)
    gathered = reduce_gradients(stacked).reshape(2, padded_rows, lanes)[:, :rows_total]
    kernel_shape = (3, 3, 3, share, lanes)
    summed_first = gathered[0].reshape(kernel_shape)
    summed_down = gathered[1].reshape(kernel_shape)
    return (encoded[None], summed_first, summed_down)


def swap(value, axis, bit):
    return lax.ppermute(value, axis, [(i, i ^ bit) for i in range(lax.axis_size(axis))])


def swap_rows(value, bits):
    count = lax.axis_size("height")
    pairs = []
    for group in range(lax.axis_size("dp")):
        bit = bits[group % 2]
        pairs += [(group * count + i, group * count + (i ^ bit)) for i in range(count)]
    return lax.ppermute(value, ("dp", "height"), pairs)


def bits_of(count):
    return [1 << k for k in range(count.bit_length() - 1)]


def split_bit(blocks, names, name, high):
    place = names.index(name)
    mine = lax.dynamic_index_in_dim(blocks, high, place, keepdims=False)
    other = lax.dynamic_index_in_dim(blocks, 1 - high, place, keepdims=False)
    return mine, other, names[:place] + names[place + 1 :]


def reduce_gradients(stacked):
    dp_bits = bits_of(lax.axis_size("dp"))
    row_bits = bits_of(lax.axis_size("height"))
    frame_bits = bits_of(lax.axis_size("tm"))
    names = [("dp", bit) for bit in reversed(dp_bits)] + [("height", bit) for bit in reversed(row_bits)]
    blocks = stacked.reshape((2,) * len(names) + (-1, 128))
    for bit in dp_bits[:-1]:
        high = (lax.axis_index("dp") // bit) % 2
        mine, other, names = split_bit(blocks, names, ("dp", bit), high)
        blocks = mine + swap(other, "dp", bit)
    near = row_bits[0::2] + row_bits[1::2]
    crossed = [near[k ^ 1] if (k ^ 1) < len(near) else near[k] for k in range(len(near))]
    stages = list(zip(near, crossed))
    core = lax.axis_index("dp") % 2
    row = lax.axis_index("height")
    held = [names, names]
    for bits in stages:
        parts = []
        for variant in (0, 1):
            high = (row // bits[variant]) % 2
            mine, other, held[variant] = split_bit(blocks, held[variant], ("height", bits[variant]), high)
            parts.append((mine, other))
        mine = jnp.where(core == 0, parts[0][0], parts[1][0])
        other = jnp.where(core == 0, parts[0][1], parts[1][1])
        blocks = mine + swap_rows(other, bits)
    far = dp_bits[-1]
    high = (lax.axis_index("dp") // far) % 2
    mine, other, _ = split_bit(blocks, held[0], ("dp", far), high)
    blocks = mine + swap(other, "dp", far)
    for bit in frame_bits:
        blocks = blocks + swap(blocks, "tm", bit)
    piece = blocks.astype(jnp.bfloat16)
    present = [[], []]
    for bits in reversed(stages):
        other = swap_rows(piece, bits)
        options = []
        for variant in (0, 1):
            bit = bits[variant]
            high = (row // bit) % 2
            place = sum(1 for kept in present[variant] if kept > bit)
            low_first = jnp.stack([piece, other], axis=place)
            high_first = jnp.stack([other, piece], axis=place)
            options.append(jnp.where(high == 0, low_first, high_first))
            present[variant].append(bit)
        piece = jnp.where(core == 0, options[0], options[1])
    return piece


def solution(mesh):
    in_specs = (
        P("dp", "tm", "height", None, None),
        P("dp", None),
        P(),
        P(),
        P("dp", "tm", "height", None, None),
    )
    out_specs = (
        P("dp", "tm", "height", None, None),
        P(None, None, None, "dp", None),
        P(None, None, None, "dp", None),
    )
    return jax.shard_map(body, mesh=mesh, in_specs=in_specs, out_specs=out_specs, check_vma=False)
```

```python
import math

import jax
import jax.numpy as jnp
from jax import lax
from jax.sharding import PartitionSpec as P


def padded_2(cells, sides, width):
    for axis, dim in sides:
        count = lax.axis_size(axis)
        ends = count - 1
        head = lax.slice_in_dim(cells, 0, width, axis=dim)
        tail = lax.slice_in_dim(cells, cells.shape[dim] - width, cells.shape[dim], axis=dim)
        cells = jnp.concatenate(
            [
                lax.ppermute(tail, axis, [(i, (i + 1) % count) for i in range(ends)]),
                cells,
                lax.ppermute(head, axis, [((i + 1) % count, i) for i in range(ends)]),
            ],
            axis=dim,
        )
    return cells


def shifted(value, axis, steps):
    count = lax.axis_size(axis)
    leading, last = (max(0, -steps), min(count, count - steps))
    return lax.ppermute(value, axis, [(source, source + steps) for source in range(leading, last)])


def conv_layer(extended, weight, tap_mask, out_frames, stride, pad_cols):
    summed = None
    for tap_time in range(3):
        frame_slab = extended[tap_time : tap_time + stride * (out_frames - 1) + 1 : stride]
        tap_term = lax.conv_general_dilated(
            frame_slab,
            weight[tap_time],
            (stride, stride),
            ((0, 0), pad_cols),
            dimension_numbers=("NHWC", "HWIO", "NHWC"),
            preferred_element_type=jnp.float32,
        )
        tap_term = tap_term * tap_mask[:, tap_time][:, None, None, None]
        summed = tap_term if summed is None else summed + tap_term
    return summed


def weight_grad(extended, grads, tap_mask, stride, pad_cols):
    out_frames = grads.shape[0]
    blocks = []
    for tap_time in range(3):
        frame_slab = extended[tap_time : tap_time + stride * (out_frames - 1) + 1 : stride]
        masked = grads * tap_mask[:, tap_time].astype(jnp.bfloat16)[:, None, None, None]
        blocks.append(
            lax.conv_general_dilated(
                frame_slab,
                masked,
                (1, 1),
                ((0, 0), pad_cols),
                rhs_dilation=(stride, stride),
                dimension_numbers=("CHWN", "IHWO", "HWNC"),
                preferred_element_type=jnp.float32,
            )
        )
    return jnp.stack(blocks)


def hidden_grad(grads_ext, weight, mask_ext):
    pieces = []
    for tap_time in range(3):
        masked = grads_ext * mask_ext[:, tap_time].astype(jnp.bfloat16)[:, None, None, None]
        kernel = jnp.transpose(weight[tap_time][::-1, ::-1], (0, 1, 3, 2))
        spread = lax.conv_general_dilated(
            masked,
            kernel,
            (1, 1),
            ((2, 0), (2, 2)),
            lhs_dilation=(2, 2),
            dimension_numbers=("NHWC", "HWIO", "NHWC"),
            preferred_element_type=jnp.float32,
        )
        pieces.append(spread[:, 1:, 1:])
    even_frames = pieces[2][:-1] + pieces[0][1:]
    odd_frames = pieces[1][1:]
    merged = jnp.stack([even_frames, odd_frames], axis=1)
    return merged.reshape((2 * even_frames.shape[0],) + even_frames.shape[1:])


def positions(counts_row, frame_index):
    starts = jnp.cumsum(counts_row) - counts_row
    latest = jnp.max(jnp.where(starts[None, :] <= frame_index[:, None], starts[None, :], 0), axis=1)
    return frame_index - latest


def tap_masks(place):
    return (place[:, None] >= (2 - jnp.arange(3, dtype=jnp.int32))[None, :]).astype(jnp.float32)


def body(clips, frame_counts, conv_first, conv_down, out_cotangent):
    frames_dev = clips.shape[1]
    rows_dev = clips.shape[2]
    columns_all = clips.shape[3]
    down_frames = frames_dev // 2
    counts_row = frame_counts[0]
    first_frame = lax.axis_index("tm") * frames_dev
    frame_index = first_frame + jnp.arange(frames_dev, dtype=jnp.int32)
    first_mask = tap_masks(positions(counts_row, frame_index))
    down_index = first_frame + 2 * jnp.arange(down_frames + 1, dtype=jnp.int32)
    mask_ext = tap_masks(positions(counts_row, down_index))
    down_mask = mask_ext[:down_frames]
    with_rows = padded_2(clips[0], (("height", 1),), 1)
    earlier = shifted(with_rows, "tm", 1)
    input_ext = jnp.concatenate([earlier, with_rows], axis=0)
    pre_act = conv_layer(input_ext, conv_first, first_mask, frames_dev, 1, (1, 1))
    hidden = jax.nn.silu(pre_act).astype(jnp.bfloat16)
    above = shifted(hidden[:, rows_dev - 1 :], "height", 1)
    hidden_rows = jnp.concatenate([above, hidden], axis=1)
    hidden_past = shifted(hidden_rows, "tm", 1)
    hidden_ext = jnp.concatenate([hidden_past, hidden_rows], axis=0)
    encoded = conv_layer(hidden_ext, conv_down, down_mask, down_frames, 2, (1, 0)).astype(
        jnp.bfloat16
    )
    cells_all = (
        lax.axis_size("dp")
        * clips.shape[0]
        * down_frames
        * lax.axis_size("tm")
        * (rows_dev // 2)
        * lax.axis_size("height")
        * (columns_all // 2)
    )
    scale = 1.0 / math.sqrt(cells_all)
    grads = (out_cotangent[0].astype(jnp.float32) * scale).astype(jnp.bfloat16)
    down_local = weight_grad(hidden_ext, grads, down_mask, 2, (1, 0))
    below = shifted(grads[:, 0:1], "height", -1)
    grads_rows = jnp.concatenate([grads, below], axis=1)
    grads_next = shifted(grads_rows, "tm", -1)
    grads_ext = jnp.concatenate([grads_rows, grads_next], axis=0)
    back_hidden = hidden_grad(grads_ext, conv_down, mask_ext).astype(jnp.bfloat16)
    sigma = jax.nn.sigmoid(pre_act)
    pre_grad = (back_hidden.astype(jnp.float32) * sigma * (1.0 + pre_act * (1.0 - sigma))).astype(
        jnp.bfloat16
    )
    first_local = weight_grad(input_ext, pre_grad, first_mask, 1, (1, 1))
    share = conv_first.shape[3] // lax.axis_size("dp")
    quarters = lax.axis_size("dp")

    lanes = conv_first.shape[-1]
    rows_total = 27 * share
    chunks = lax.axis_size("height") // 2
    chunk_rows = -(-rows_total // (chunks * 16)) * 16
    padded_rows = chunk_rows * chunks

    def by_quarter(term):
        term = term.reshape(27, quarters, share, lanes)
        term = jnp.transpose(term, (1, 0, 2, 3)).reshape(quarters, rows_total, lanes)
        return jnp.pad(term, ((0, 0), (0, padded_rows - rows_total), (0, 0)))

    stacked = jnp.stack([by_quarter(first_local), by_quarter(down_local)], axis=1)
    gathered = reduce_gradients(stacked).reshape(2, padded_rows, lanes)[:, :rows_total]
    kernel_shape = (3, 3, 3, share, lanes)
    summed_first = gathered[0].reshape(kernel_shape)
    summed_down = gathered[1].reshape(kernel_shape)
    return (encoded[None], summed_first, summed_down)


def swap(value, axis, bit):
    return lax.ppermute(value, axis, [(i, i ^ bit) for i in range(lax.axis_size(axis))])


def swap_rows(value, bits):
    count = lax.axis_size("height")
    pairs = []
    for group in range(lax.axis_size("dp")):
        bit = bits[group % 2]
        pairs += [(group * count + i, group * count + (i ^ bit)) for i in range(count)]
    return lax.ppermute(value, ("dp", "height"), pairs)


def bits_of(count):
    return [1 << k for k in range(count.bit_length() - 1)]


def split_bit(blocks, names, name, high):
    place = names.index(name)
    mine = lax.dynamic_index_in_dim(blocks, high, place, keepdims=False)
    other = lax.dynamic_index_in_dim(blocks, 1 - high, place, keepdims=False)
    return mine, other, names[:place] + names[place + 1 :]


def reduce_gradients(stacked):
    dp_bits = bits_of(lax.axis_size("dp"))
    row_bits = bits_of(lax.axis_size("height"))
    frame_bits = bits_of(lax.axis_size("tm"))
    names = [("dp", bit) for bit in reversed(dp_bits)] + [("height", bit) for bit in reversed(row_bits)]
    blocks = stacked.reshape((2,) * len(names) + (-1, 128))
    for bit in dp_bits[:-1]:
        high = (lax.axis_index("dp") // bit) % 2
        mine, other, names = split_bit(blocks, names, ("dp", bit), high)
        blocks = mine + swap(other, "dp", bit)
    near = row_bits[0::2] + row_bits[1::2]
    crossed = [near[k ^ 1] if (k ^ 1) < len(near) else near[k] for k in range(len(near))]
    stages = list(zip(near, crossed))
    core = lax.axis_index("dp") % 2
    row = lax.axis_index("height")
    held = [names, names]
    for bits in stages:
        parts = []
        for variant in (0, 1):
            high = (row // bits[variant]) % 2
            mine, other, held[variant] = split_bit(blocks, held[variant], ("height", bits[variant]), high)
            parts.append((mine, other))
        mine = jnp.where(core == 0, parts[0][0], parts[1][0])
        other = jnp.where(core == 0, parts[0][1], parts[1][1])
        blocks = mine + swap_rows(other, bits)
    far = dp_bits[-1]
    high = (lax.axis_index("dp") // far) % 2
    mine, other, _ = split_bit(blocks, held[0], ("dp", far), high)
    blocks = mine + swap(other, "dp", far)
    for bit in frame_bits:
        blocks = blocks + swap(blocks, "tm", bit)
    piece = blocks.astype(jnp.bfloat16)
    return lax.all_gather(piece, "height", axis=0, tiled=False)


def solution(mesh):
    in_specs = (
        P("dp", "tm", "height", None, None),
        P("dp", None),
        P(),
        P(),
        P("dp", "tm", "height", None, None),
    )
    out_specs = (
        P("dp", "tm", "height", None, None),
        P(None, None, None, "dp", None),
        P(None, None, None, "dp", None),
    )
    return jax.shard_map(body, mesh=mesh, in_specs=in_specs, out_specs=out_specs, check_vma=False)
```

```python
import math

import jax
import jax.numpy as jnp
from jax import lax
from jax.sharding import PartitionSpec as P


def padded_2(cells, sides, width):
    for axis, dim in sides:
        count = lax.axis_size(axis)
        ends = count - 1
        head = lax.slice_in_dim(cells, 0, width, axis=dim)
        tail = lax.slice_in_dim(cells, cells.shape[dim] - width, cells.shape[dim], axis=dim)
        cells = jnp.concatenate(
            [
                lax.ppermute(tail, axis, [(i, (i + 1) % count) for i in range(ends)]),
                cells,
                lax.ppermute(head, axis, [((i + 1) % count, i) for i in range(ends)]),
            ],
            axis=dim,
        )
    return cells


def shifted(value, axis, steps):
    count = lax.axis_size(axis)
    leading, last = (max(0, -steps), min(count, count - steps))
    return lax.ppermute(value, axis, [(source, source + steps) for source in range(leading, last)])


def conv_layer(extended, weight, tap_mask, out_frames, stride, pad_cols):
    summed = None
    for tap_time in range(3):
        frame_slab = extended[tap_time : tap_time + stride * (out_frames - 1) + 1 : stride]
        tap_term = lax.conv_general_dilated(
            frame_slab,
            weight[tap_time],
            (stride, stride),
            ((0, 0), pad_cols),
            dimension_numbers=("NHWC", "HWIO", "NHWC"),
            preferred_element_type=jnp.float32,
        )
        tap_term = tap_term * tap_mask[:, tap_time][:, None, None, None]
        summed = tap_term if summed is None else summed + tap_term
    return summed


def weight_grad(extended, grads, tap_mask, stride, pad_cols):
    out_frames = grads.shape[0]
    blocks = []
    for tap_time in range(3):
        frame_slab = extended[tap_time : tap_time + stride * (out_frames - 1) + 1 : stride]
        masked = grads * tap_mask[:, tap_time].astype(jnp.bfloat16)[:, None, None, None]
        blocks.append(
            lax.conv_general_dilated(
                frame_slab,
                masked,
                (1, 1),
                ((0, 0), pad_cols),
                rhs_dilation=(stride, stride),
                dimension_numbers=("CHWN", "IHWO", "HWNC"),
                preferred_element_type=jnp.float32,
            )
        )
    return jnp.stack(blocks)


def hidden_grad(grads_ext, weight, mask_ext):
    pieces = []
    for tap_time in range(3):
        masked = grads_ext * mask_ext[:, tap_time].astype(jnp.bfloat16)[:, None, None, None]
        kernel = jnp.transpose(weight[tap_time][::-1, ::-1], (0, 1, 3, 2))
        spread = lax.conv_general_dilated(
            masked,
            kernel,
            (1, 1),
            ((2, 0), (2, 2)),
            lhs_dilation=(2, 2),
            dimension_numbers=("NHWC", "HWIO", "NHWC"),
            preferred_element_type=jnp.float32,
        )
        pieces.append(spread[:, 1:, 1:])
    even_frames = pieces[2][:-1] + pieces[0][1:]
    odd_frames = pieces[1][1:]
    merged = jnp.stack([even_frames, odd_frames], axis=1)
    return merged.reshape((2 * even_frames.shape[0],) + even_frames.shape[1:])


def positions(counts_row, frame_index):
    starts = jnp.cumsum(counts_row) - counts_row
    latest = jnp.max(jnp.where(starts[None, :] <= frame_index[:, None], starts[None, :], 0), axis=1)
    return frame_index - latest


def tap_masks(place):
    return (place[:, None] >= (2 - jnp.arange(3, dtype=jnp.int32))[None, :]).astype(jnp.float32)


def body(clips, frame_counts, conv_first, conv_down, out_cotangent):
    frames_dev = clips.shape[1]
    rows_dev = clips.shape[2]
    columns_all = clips.shape[3]
    down_frames = frames_dev // 2
    counts_row = frame_counts[0]
    first_frame = lax.axis_index("tm") * frames_dev
    frame_index = first_frame + jnp.arange(frames_dev, dtype=jnp.int32)
    first_mask = tap_masks(positions(counts_row, frame_index))
    down_index = first_frame + 2 * jnp.arange(down_frames + 1, dtype=jnp.int32)
    mask_ext = tap_masks(positions(counts_row, down_index))
    down_mask = mask_ext[:down_frames]
    with_rows = padded_2(clips[0], (("height", 1),), 1)
    earlier = shifted(with_rows, "tm", 1)
    input_ext = jnp.concatenate([earlier, with_rows], axis=0)
    pre_act = conv_layer(input_ext, conv_first, first_mask, frames_dev, 1, (1, 1))
    hidden = jax.nn.silu(pre_act).astype(jnp.bfloat16)
    above = shifted(hidden[:, rows_dev - 1 :], "height", 1)
    hidden_rows = jnp.concatenate([above, hidden], axis=1)
    hidden_past = shifted(hidden_rows, "tm", 1)
    hidden_ext = jnp.concatenate([hidden_past, hidden_rows], axis=0)
    encoded = conv_layer(hidden_ext, conv_down, down_mask, down_frames, 2, (1, 0)).astype(
        jnp.bfloat16
    )
    cells_all = (
        lax.axis_size("dp")
        * clips.shape[0]
        * down_frames
        * lax.axis_size("tm")
        * (rows_dev // 2)
        * lax.axis_size("height")
        * (columns_all // 2)
    )
    scale = 1.0 / math.sqrt(cells_all)
    grads = (out_cotangent[0].astype(jnp.float32) * scale).astype(jnp.bfloat16)
    down_local = weight_grad(hidden_ext, grads, down_mask, 2, (1, 0))
    below = shifted(grads[:, 0:1], "height", -1)
    grads_rows = jnp.concatenate([grads, below], axis=1)
    grads_next = shifted(grads_rows, "tm", -1)
    grads_ext = jnp.concatenate([grads_rows, grads_next], axis=0)
    back_hidden = hidden_grad(grads_ext, conv_down, mask_ext).astype(jnp.bfloat16)
    sigma = jax.nn.sigmoid(pre_act)
    pre_grad = (back_hidden.astype(jnp.float32) * sigma * (1.0 + pre_act * (1.0 - sigma))).astype(
        jnp.bfloat16
    )
    first_local = weight_grad(input_ext, pre_grad, first_mask, 1, (1, 1))
    share = conv_first.shape[3] // lax.axis_size("dp")
    quarters = lax.axis_size("dp")

    lanes = conv_first.shape[-1]
    rows_total = 27 * share
    chunks = lax.axis_size("height") // 2
    chunk_rows = -(-rows_total // (chunks * 16)) * 16
    padded_rows = chunk_rows * chunks

    def by_quarter(term):
        term = term.reshape(27, quarters, share, lanes)
        term = jnp.transpose(term, (1, 0, 2, 3)).reshape(quarters, rows_total, lanes)
        return jnp.pad(term, ((0, 0), (0, padded_rows - rows_total), (0, 0)))

    stacked = jnp.stack([by_quarter(first_local), by_quarter(down_local)], axis=1)
    gathered = reduce_gradients(stacked).reshape(2, padded_rows, lanes)[:, :rows_total]
    kernel_shape = (3, 3, 3, share, lanes)
    summed_first = gathered[0].reshape(kernel_shape)
    summed_down = gathered[1].reshape(kernel_shape)
    return (encoded[None], summed_first, summed_down)


def swap(value, axis, bit):
    return lax.ppermute(value, axis, [(i, i ^ bit) for i in range(lax.axis_size(axis))])


def swap_rows(value, bits):
    count = lax.axis_size("height")
    pairs = []
    for group in range(lax.axis_size("dp")):
        bit = bits[group % 2]
        pairs += [(group * count + i, group * count + (i ^ bit)) for i in range(count)]
    return lax.ppermute(value, ("dp", "height"), pairs)


def bits_of(count):
    return [1 << k for k in range(count.bit_length() - 1)]


def split_bit(blocks, names, name, high):
    place = names.index(name)
    mine = lax.dynamic_index_in_dim(blocks, high, place, keepdims=False)
    other = lax.dynamic_index_in_dim(blocks, 1 - high, place, keepdims=False)
    return mine, other, names[:place] + names[place + 1 :]


def reduce_gradients(stacked):
    dp_bits = bits_of(lax.axis_size("dp"))
    row_bits = bits_of(lax.axis_size("height"))
    frame_bits = bits_of(lax.axis_size("tm"))
    names = [("dp", bit) for bit in reversed(dp_bits)] + [("height", bit) for bit in reversed(row_bits)]
    blocks = stacked.reshape((2,) * len(names) + (-1, 128))
    for bit in dp_bits[:-1]:
        high = (lax.axis_index("dp") // bit) % 2
        mine, other, names = split_bit(blocks, names, ("dp", bit), high)
        blocks = mine + swap(other, "dp", bit)
    near = row_bits[0::2] + row_bits[1::2]
    crossed = [near[k ^ 1] if (k ^ 1) < len(near) else near[k] for k in range(len(near))]
    stages = list(zip(near, crossed))
    core = lax.axis_index("dp") % 2
    row = lax.axis_index("height")
    held = [names, names]
    for bits in stages:
        parts = []
        for variant in (0, 1):
            high = (row // bits[variant]) % 2
            mine, other, held[variant] = split_bit(blocks, held[variant], ("height", bits[variant]), high)
            parts.append((mine, other))
        mine = jnp.where(core == 0, parts[0][0], parts[1][0])
        other = jnp.where(core == 0, parts[0][1], parts[1][1])
        blocks = mine + swap_rows(other, bits)
    for bit in frame_bits:
        blocks = blocks + swap(blocks, "tm", bit)
    far, top = dp_bits[-1], frame_bits[-1]
    frames = lax.axis_size("tm")
    high = (lax.axis_index("dp") // far) % 2
    mine, other, _ = split_bit(blocks, held[0], ("dp", far), high)
    pairs = [
        (group * frames + t, (group ^ far) * frames + (t ^ top))
        for group in range(lax.axis_size("dp"))
        for t in range(frames)
    ]
    piece = (mine + lax.ppermute(other, ("dp", "tm"), pairs)).astype(jnp.bfloat16)
    return lax.all_gather(piece, "height", axis=0, tiled=False)


def solution(mesh):
    in_specs = (
        P("dp", "tm", "height", None, None),
        P("dp", None),
        P(),
        P(),
        P("dp", "tm", "height", None, None),
    )
    out_specs = (
        P("dp", "tm", "height", None, None),
        P(None, None, None, "dp", None),
        P(None, None, None, "dp", None),
    )
    return jax.shard_map(body, mesh=mesh, in_specs=in_specs, out_specs=out_specs, check_vma=False)
```

```python
import math

import jax
import jax.numpy as jnp
from jax import lax
from jax.sharding import PartitionSpec as P


def padded_2(cells, sides, width):
    for axis, dim in sides:
        count = lax.axis_size(axis)
        ends = count - 1
        head = lax.slice_in_dim(cells, 0, width, axis=dim)
        tail = lax.slice_in_dim(cells, cells.shape[dim] - width, cells.shape[dim], axis=dim)
        cells = jnp.concatenate(
            [
                lax.ppermute(tail, axis, [(i, (i + 1) % count) for i in range(ends)]),
                cells,
                lax.ppermute(head, axis, [((i + 1) % count, i) for i in range(ends)]),
            ],
            axis=dim,
        )
    return cells


def shifted(value, axis, steps):
    count = lax.axis_size(axis)
    leading, last = (max(0, -steps), min(count, count - steps))
    return lax.ppermute(value, axis, [(source, source + steps) for source in range(leading, last)])


def conv_layer(extended, weight, tap_mask, out_frames, stride, pad_cols):
    summed = None
    for tap_time in range(3):
        frame_slab = extended[tap_time : tap_time + stride * (out_frames - 1) + 1 : stride]
        tap_term = lax.conv_general_dilated(
            frame_slab,
            weight[tap_time],
            (stride, stride),
            ((0, 0), pad_cols),
            dimension_numbers=("NHWC", "HWIO", "NHWC"),
            preferred_element_type=jnp.float32,
        )
        tap_term = tap_term * tap_mask[:, tap_time][:, None, None, None]
        summed = tap_term if summed is None else summed + tap_term
    return summed


def weight_grad(extended, grads, tap_mask, stride, pad_cols):
    out_frames = grads.shape[0]
    blocks = []
    for tap_time in range(3):
        frame_slab = extended[tap_time : tap_time + stride * (out_frames - 1) + 1 : stride]
        masked = grads * tap_mask[:, tap_time].astype(jnp.bfloat16)[:, None, None, None]
        blocks.append(
            lax.conv_general_dilated(
                frame_slab,
                masked,
                (1, 1),
                ((0, 0), pad_cols),
                rhs_dilation=(stride, stride),
                dimension_numbers=("CHWN", "IHWO", "HWNC"),
                preferred_element_type=jnp.float32,
            )
        )
    return jnp.stack(blocks)


def hidden_grad(grads_ext, weight, mask_ext):
    pieces = []
    for tap_time in range(3):
        masked = grads_ext * mask_ext[:, tap_time].astype(jnp.bfloat16)[:, None, None, None]
        kernel = jnp.transpose(weight[tap_time][::-1, ::-1], (0, 1, 3, 2))
        spread = lax.conv_general_dilated(
            masked,
            kernel,
            (1, 1),
            ((2, 0), (2, 2)),
            lhs_dilation=(2, 2),
            dimension_numbers=("NHWC", "HWIO", "NHWC"),
            preferred_element_type=jnp.float32,
        )
        pieces.append(spread[:, 1:, 1:])
    even_frames = pieces[2][:-1] + pieces[0][1:]
    odd_frames = pieces[1][1:]
    merged = jnp.stack([even_frames, odd_frames], axis=1)
    return merged.reshape((2 * even_frames.shape[0],) + even_frames.shape[1:])


def positions(counts_row, frame_index):
    starts = jnp.cumsum(counts_row) - counts_row
    latest = jnp.max(jnp.where(starts[None, :] <= frame_index[:, None], starts[None, :], 0), axis=1)
    return frame_index - latest


def tap_masks(place):
    return (place[:, None] >= (2 - jnp.arange(3, dtype=jnp.int32))[None, :]).astype(jnp.float32)


def body(clips, frame_counts, conv_first, conv_down, out_cotangent):
    frames_dev = clips.shape[1]
    rows_dev = clips.shape[2]
    columns_all = clips.shape[3]
    down_frames = frames_dev // 2
    counts_row = frame_counts[0]
    first_frame = lax.axis_index("tm") * frames_dev
    wide_index = first_frame - 2 + jnp.arange(frames_dev + 2, dtype=jnp.int32)
    wide_mask = tap_masks(positions(counts_row, wide_index))
    first_mask = wide_mask[2:]
    down_index = first_frame + 2 * jnp.arange(down_frames + 1, dtype=jnp.int32)
    mask_ext = tap_masks(positions(counts_row, down_index))
    down_mask = mask_ext[:down_frames]
    cells = clips[0]
    above = shifted(cells[:, rows_dev - 2 :], "height", 1)
    below = shifted(cells[:, :1], "height", -1)
    with_rows = jnp.concatenate([above, cells, below], axis=1)
    if frames_dev >= 4:
        earlier = shifted(with_rows[frames_dev - 4 :], "tm", 1)
    else:
        earlier = jnp.concatenate([shifted(with_rows, "tm", 2), shifted(with_rows, "tm", 1)], axis=0)
    wide_input = jnp.concatenate([earlier, with_rows], axis=0)
    wide_pre = conv_layer(wide_input, conv_first, wide_mask, frames_dev + 2, 1, (1, 1))
    row_valid = jnp.arange(rows_dev + 1) >= jnp.where(lax.axis_index("height") == 0, 1, 0)
    hidden_ext = jnp.where(
        row_valid[None, :, None, None], jax.nn.silu(wide_pre).astype(jnp.bfloat16), 0
    ).astype(jnp.bfloat16)
    pre_act = wide_pre[2:, 1:]
    input_ext = wide_input[2:, 1:]
    encoded = conv_layer(hidden_ext, conv_down, down_mask, down_frames, 2, (1, 0)).astype(
        jnp.bfloat16
    )
    cells_all = (
        lax.axis_size("dp")
        * clips.shape[0]
        * down_frames
        * lax.axis_size("tm")
        * (rows_dev // 2)
        * lax.axis_size("height")
        * (columns_all // 2)
    )
    scale = 1.0 / math.sqrt(cells_all)
    grads = (out_cotangent[0].astype(jnp.float32) * scale).astype(jnp.bfloat16)
    down_local = weight_grad(hidden_ext, grads, down_mask, 2, (1, 0))
    below = shifted(grads[:, 0:1], "height", -1)
    grads_rows = jnp.concatenate([grads, below], axis=1)
    grads_next = shifted(grads_rows, "tm", -1)
    grads_ext = jnp.concatenate([grads_rows, grads_next], axis=0)
    back_hidden = hidden_grad(grads_ext, conv_down, mask_ext).astype(jnp.bfloat16)
    sigma = jax.nn.sigmoid(pre_act)
    pre_grad = (back_hidden.astype(jnp.float32) * sigma * (1.0 + pre_act * (1.0 - sigma))).astype(
        jnp.bfloat16
    )
    first_local = weight_grad(input_ext, pre_grad, first_mask, 1, (1, 1))
    share = conv_first.shape[3] // lax.axis_size("dp")
    quarters = lax.axis_size("dp")

    lanes = conv_first.shape[-1]
    rows_total = 27 * share
    chunks = lax.axis_size("height") // 2
    chunk_rows = -(-rows_total // (chunks * 16)) * 16
    padded_rows = chunk_rows * chunks

    def by_quarter(term):
        term = term.reshape(27, quarters, share, lanes)
        term = jnp.transpose(term, (1, 0, 2, 3)).reshape(quarters, rows_total, lanes)
        return jnp.pad(term, ((0, 0), (0, padded_rows - rows_total), (0, 0)))

    stacked = jnp.stack([by_quarter(first_local), by_quarter(down_local)], axis=1)
    gathered = reduce_gradients(stacked).reshape(2, padded_rows, lanes)[:, :rows_total]
    kernel_shape = (3, 3, 3, share, lanes)
    summed_first = gathered[0].reshape(kernel_shape)
    summed_down = gathered[1].reshape(kernel_shape)
    return (encoded[None], summed_first, summed_down)


def swap(value, axis, bit):
    return lax.ppermute(value, axis, [(i, i ^ bit) for i in range(lax.axis_size(axis))])


def swap_rows(value, bits):
    count = lax.axis_size("height")
    pairs = []
    for group in range(lax.axis_size("dp")):
        bit = bits[group % 2]
        pairs += [(group * count + i, group * count + (i ^ bit)) for i in range(count)]
    return lax.ppermute(value, ("dp", "height"), pairs)


def bits_of(count):
    return [1 << k for k in range(count.bit_length() - 1)]


def split_bit(blocks, names, name, high):
    place = names.index(name)
    mine = lax.dynamic_index_in_dim(blocks, high, place, keepdims=False)
    other = lax.dynamic_index_in_dim(blocks, 1 - high, place, keepdims=False)
    return mine, other, names[:place] + names[place + 1 :]


def reduce_gradients(stacked):
    dp_bits = bits_of(lax.axis_size("dp"))
    row_bits = bits_of(lax.axis_size("height"))
    frame_bits = bits_of(lax.axis_size("tm"))
    names = [("dp", bit) for bit in reversed(dp_bits)] + [("height", bit) for bit in reversed(row_bits)]
    blocks = stacked.reshape((2,) * len(names) + (-1, 128))
    for bit in dp_bits[:-1]:
        high = (lax.axis_index("dp") // bit) % 2
        mine, other, names = split_bit(blocks, names, ("dp", bit), high)
        blocks = mine + swap(other, "dp", bit)
    near = row_bits[0::2] + row_bits[1::2]
    crossed = [near[k ^ 1] if (k ^ 1) < len(near) else near[k] for k in range(len(near))]
    stages = list(zip(near, crossed))
    core = lax.axis_index("dp") % 2
    row = lax.axis_index("height")
    held = [names, names]
    for bits in stages:
        parts = []
        for variant in (0, 1):
            high = (row // bits[variant]) % 2
            mine, other, held[variant] = split_bit(blocks, held[variant], ("height", bits[variant]), high)
            parts.append((mine, other))
        mine = jnp.where(core == 0, parts[0][0], parts[1][0])
        other = jnp.where(core == 0, parts[0][1], parts[1][1])
        blocks = mine + swap_rows(other, bits)
    far = dp_bits[-1]
    high = (lax.axis_index("dp") // far) % 2
    mine, other, _ = split_bit(blocks, held[0], ("dp", far), high)
    blocks = mine + swap(other, "dp", far)
    for bit in frame_bits:
        blocks = blocks + swap(blocks, "tm", bit)
    piece = blocks.astype(jnp.bfloat16)
    return lax.all_gather(piece, "height", axis=0, tiled=False)


def solution(mesh):
    in_specs = (
        P("dp", "tm", "height", None, None),
        P("dp", None),
        P(),
        P(),
        P("dp", "tm", "height", None, None),
    )
    out_specs = (
        P("dp", "tm", "height", None, None),
        P(None, None, None, "dp", None),
        P(None, None, None, "dp", None),
    )
    return jax.shard_map(body, mesh=mesh, in_specs=in_specs, out_specs=out_specs, check_vma=False)
```

```python
import math

import jax
import numpy as np
import jax.numpy as jnp
from jax import lax
from jax.sharding import PartitionSpec as P


def padded_2(cells, sides, width):
    for axis, dim in sides:
        count = lax.axis_size(axis)
        ends = count - 1
        head = lax.slice_in_dim(cells, 0, width, axis=dim)
        tail = lax.slice_in_dim(cells, cells.shape[dim] - width, cells.shape[dim], axis=dim)
        cells = jnp.concatenate(
            [
                lax.ppermute(tail, axis, [(i, (i + 1) % count) for i in range(ends)]),
                cells,
                lax.ppermute(head, axis, [((i + 1) % count, i) for i in range(ends)]),
            ],
            axis=dim,
        )
    return cells


def shifted(value, axis, steps):
    count = lax.axis_size(axis)
    leading, last = (max(0, -steps), min(count, count - steps))
    return lax.ppermute(value, axis, [(source, source + steps) for source in range(leading, last)])


def conv_layer(extended, weight, tap_mask, out_frames, stride, pad_cols):
    summed = None
    for tap_time in range(3):
        frame_slab = extended[tap_time : tap_time + stride * (out_frames - 1) + 1 : stride]
        tap_term = lax.conv_general_dilated(
            frame_slab,
            weight[tap_time],
            (stride, stride),
            ((0, 0), pad_cols),
            dimension_numbers=("NHWC", "HWIO", "NHWC"),
            preferred_element_type=jnp.float32,
        )
        tap_term = tap_term * tap_mask[:, tap_time][:, None, None, None]
        summed = tap_term if summed is None else summed + tap_term
    return summed


def weight_grad(extended, grads, tap_mask, stride, pad_cols):
    out_frames = grads.shape[0]
    blocks = []
    for tap_time in range(3):
        frame_slab = extended[tap_time : tap_time + stride * (out_frames - 1) + 1 : stride]
        masked = grads * tap_mask[:, tap_time].astype(jnp.bfloat16)[:, None, None, None]
        blocks.append(
            lax.conv_general_dilated(
                frame_slab,
                masked,
                (1, 1),
                ((0, 0), pad_cols),
                rhs_dilation=(stride, stride),
                dimension_numbers=("CHWN", "IHWO", "HWNC"),
                preferred_element_type=jnp.float32,
            )
        )
    return jnp.stack(blocks)


def hidden_grad(grads_ext, weight, mask_ext):
    pieces = []
    for tap_time in range(3):
        masked = grads_ext * mask_ext[:, tap_time].astype(jnp.bfloat16)[:, None, None, None]
        kernel = jnp.transpose(weight[tap_time][::-1, ::-1], (0, 1, 3, 2))
        spread = lax.conv_general_dilated(
            masked,
            kernel,
            (1, 1),
            ((2, 0), (2, 2)),
            lhs_dilation=(2, 2),
            dimension_numbers=("NHWC", "HWIO", "NHWC"),
            preferred_element_type=jnp.float32,
        )
        pieces.append(spread[:, 1:, 1:])
    even_frames = pieces[2][:-1] + pieces[0][1:]
    odd_frames = pieces[1][1:]
    merged = jnp.stack([even_frames, odd_frames], axis=1)
    return merged.reshape((2 * even_frames.shape[0],) + even_frames.shape[1:])


def positions(counts_row, frame_index):
    starts = jnp.cumsum(counts_row) - counts_row
    latest = jnp.max(jnp.where(starts[None, :] <= frame_index[:, None], starts[None, :], 0), axis=1)
    return frame_index - latest


def tap_masks(place):
    return (place[:, None] >= (2 - jnp.arange(3, dtype=jnp.int32))[None, :]).astype(jnp.float32)


def body(clips, frame_counts, conv_first, conv_down, out_cotangent):
    frames_dev = clips.shape[1]
    rows_dev = clips.shape[2]
    columns_all = clips.shape[3]
    down_frames = frames_dev // 2
    counts_row = frame_counts[0]
    first_frame = lax.axis_index("tm") * frames_dev
    frame_index = first_frame + jnp.arange(frames_dev, dtype=jnp.int32)
    first_mask = tap_masks(positions(counts_row, frame_index))
    down_index = first_frame + 2 * jnp.arange(down_frames + 1, dtype=jnp.int32)
    mask_ext = tap_masks(positions(counts_row, down_index))
    down_mask = mask_ext[:down_frames]
    with_rows = padded_2(clips[0], (("height", 1),), 1)
    earlier = shifted(with_rows, "tm", 1)
    input_ext = jnp.concatenate([earlier, with_rows], axis=0)
    pre_act = conv_layer(input_ext, conv_first, first_mask, frames_dev, 1, (1, 1))
    hidden = jax.nn.silu(pre_act).astype(jnp.bfloat16)
    above = shifted(hidden[:, rows_dev - 1 :], "height", 1)
    hidden_rows = jnp.concatenate([above, hidden], axis=1)
    hidden_past = shifted(hidden_rows, "tm", 1)
    hidden_ext = jnp.concatenate([hidden_past, hidden_rows], axis=0)
    encoded = conv_layer(hidden_ext, conv_down, down_mask, down_frames, 2, (1, 0)).astype(
        jnp.bfloat16
    )
    cells_all = (
        lax.axis_size("dp")
        * clips.shape[0]
        * down_frames
        * lax.axis_size("tm")
        * (rows_dev // 2)
        * lax.axis_size("height")
        * (columns_all // 2)
    )
    scale = 1.0 / math.sqrt(cells_all)
    grads = (out_cotangent[0].astype(jnp.float32) * scale).astype(jnp.bfloat16)
    down_local = weight_grad(hidden_ext, grads, down_mask, 2, (1, 0))
    below = shifted(grads[:, 0:1], "height", -1)
    grads_rows = jnp.concatenate([grads, below], axis=1)
    grads_next = shifted(grads_rows, "tm", -1)
    grads_ext = jnp.concatenate([grads_rows, grads_next], axis=0)
    back_hidden = hidden_grad(grads_ext, conv_down, mask_ext).astype(jnp.bfloat16)
    sigma = jax.nn.sigmoid(pre_act)
    pre_grad = (back_hidden.astype(jnp.float32) * sigma * (1.0 + pre_act * (1.0 - sigma))).astype(
        jnp.bfloat16
    )
    first_local = weight_grad(input_ext, pre_grad, first_mask, 1, (1, 1))
    share = conv_first.shape[3] // lax.axis_size("dp")
    quarters = lax.axis_size("dp")

    lanes = conv_first.shape[-1]
    rows_total = 27 * share
    chunks = lax.axis_size("height") // 2
    chunk_rows = -(-rows_total // (chunks * 16)) * 16
    padded_rows = chunk_rows * chunks

    def by_quarter(term):
        term = term.reshape(27, quarters, share, lanes)
        term = jnp.transpose(term, (1, 0, 2, 3)).reshape(quarters, rows_total, lanes)
        return jnp.pad(term, ((0, 0), (0, padded_rows - rows_total), (0, 0)))

    stacked = jnp.stack([by_quarter(first_local), by_quarter(down_local)], axis=1)
    gathered = reduce_gradients(stacked).reshape(2, padded_rows, lanes)[:, :rows_total]
    kernel_shape = (3, 3, 3, share, lanes)
    summed_first = gathered[0].reshape(kernel_shape)
    summed_down = gathered[1].reshape(kernel_shape)
    return (encoded[None], summed_first, summed_down)


def swap(value, axis, bit):
    return lax.ppermute(value, axis, [(i, i ^ bit) for i in range(lax.axis_size(axis))])


def ring_mask(bit, low_bits):
    return bit if bit in low_bits else bit | bit // 2


def swap_rows(value, bits, low_bits):
    count = lax.axis_size("height")
    pairs = []
    for group in range(lax.axis_size("dp")):
        mask = ring_mask(bits[group % 2], low_bits)
        pairs += [(group * count + i, group * count + (i ^ mask)) for i in range(count)]
    return lax.ppermute(value, ("dp", "height"), pairs)


def kept_bit(row, bit, low_bits):
    if bit in low_bits:
        return ((row // bit) ^ (row // (2 * bit))) % 2
    return (row // bit) % 2


def bits_of(count):
    return [1 << k for k in range(count.bit_length() - 1)]


def split_bit(blocks, names, name, high):
    place = names.index(name)
    mine = lax.dynamic_index_in_dim(blocks, high, place, keepdims=False)
    other = lax.dynamic_index_in_dim(blocks, 1 - high, place, keepdims=False)
    return mine, other, names[:place] + names[place + 1 :]


def reduce_gradients(stacked):
    dp_bits = bits_of(lax.axis_size("dp"))
    row_bits = bits_of(lax.axis_size("height"))
    frame_bits = bits_of(lax.axis_size("tm"))
    names = [("dp", bit) for bit in reversed(dp_bits)] + [("height", bit) for bit in reversed(row_bits)]
    blocks = stacked.reshape((2,) * len(names) + (-1, 128))
    for bit in dp_bits[:-1]:
        high = (lax.axis_index("dp") // bit) % 2
        mine, other, names = split_bit(blocks, names, ("dp", bit), high)
        blocks = mine + swap(other, "dp", bit)
    near = row_bits[0::2] + row_bits[1::2]
    crossed = [near[k ^ 1] if (k ^ 1) < len(near) else near[k] for k in range(len(near))]
    stages = list(zip(near, crossed))
    core = lax.axis_index("dp") % 2
    row = lax.axis_index("height")
    held = [names, names]
    low_bits = row_bits[0::2]
    for bits in stages:
        parts = []
        for variant in (0, 1):
            high = kept_bit(row, bits[variant], low_bits)
            mine, other, held[variant] = split_bit(blocks, held[variant], ("height", bits[variant]), high)
            parts.append((mine, other))
        mine = jnp.where(core == 0, parts[0][0], parts[1][0])
        other = jnp.where(core == 0, parts[0][1], parts[1][1])
        blocks = mine + swap_rows(other, bits, low_bits)
    far = dp_bits[-1]
    high = (lax.axis_index("dp") // far) % 2
    mine, other, _ = split_bit(blocks, held[0], ("dp", far), high)
    blocks = mine + swap(other, "dp", far)
    for bit in frame_bits:
        blocks = blocks + swap(blocks, "tm", bit)
    piece = blocks.astype(jnp.bfloat16)
    gathered = lax.all_gather(piece, "height", axis=0, tiled=False)
    owner = [h ^ sum((h >> 1) & bit for bit in low_bits) for h in range(gathered.shape[0])]
    return gathered[np.array(owner)]


def solution(mesh):
    in_specs = (
        P("dp", "tm", "height", None, None),
        P("dp", None),
        P(),
        P(),
        P("dp", "tm", "height", None, None),
    )
    out_specs = (
        P("dp", "tm", "height", None, None),
        P(None, None, None, "dp", None),
        P(None, None, None, "dp", None),
    )
    return jax.shard_map(body, mesh=mesh, in_specs=in_specs, out_specs=out_specs, check_vma=False)
```

```python
import math

import jax
import numpy as np
import jax.numpy as jnp
from jax import lax
from jax.sharding import PartitionSpec as P


def padded_2(cells, sides, width):
    for axis, dim in sides:
        count = lax.axis_size(axis)
        ends = count - 1
        head = lax.slice_in_dim(cells, 0, width, axis=dim)
        tail = lax.slice_in_dim(cells, cells.shape[dim] - width, cells.shape[dim], axis=dim)
        cells = jnp.concatenate(
            [
                lax.ppermute(tail, axis, [(i, (i + 1) % count) for i in range(ends)]),
                cells,
                lax.ppermute(head, axis, [((i + 1) % count, i) for i in range(ends)]),
            ],
            axis=dim,
        )
    return cells


def shifted(value, axis, steps):
    count = lax.axis_size(axis)
    leading, last = (max(0, -steps), min(count, count - steps))
    return lax.ppermute(value, axis, [(source, source + steps) for source in range(leading, last)])


def conv_layer(extended, weight, tap_mask, out_frames, stride, pad_cols):
    summed = None
    for tap_time in range(3):
        frame_slab = extended[tap_time : tap_time + stride * (out_frames - 1) + 1 : stride]
        tap_term = lax.conv_general_dilated(
            frame_slab,
            weight[tap_time],
            (stride, stride),
            ((0, 0), pad_cols),
            dimension_numbers=("NHWC", "HWIO", "NHWC"),
            preferred_element_type=jnp.float32,
        )
        tap_term = tap_term * tap_mask[:, tap_time][:, None, None, None]
        summed = tap_term if summed is None else summed + tap_term
    return summed


def weight_grad(extended, grads, tap_mask, stride, pad_cols):
    out_frames = grads.shape[0]
    blocks = []
    for tap_time in range(3):
        frame_slab = extended[tap_time : tap_time + stride * (out_frames - 1) + 1 : stride]
        masked = grads * tap_mask[:, tap_time].astype(jnp.bfloat16)[:, None, None, None]
        blocks.append(
            lax.conv_general_dilated(
                frame_slab,
                masked,
                (1, 1),
                ((0, 0), pad_cols),
                rhs_dilation=(stride, stride),
                dimension_numbers=("CHWN", "IHWO", "HWNC"),
                preferred_element_type=jnp.float32,
            )
        )
    return jnp.stack(blocks)


def hidden_grad(grads_ext, weight, mask_ext):
    pieces = []
    for tap_time in range(3):
        masked = grads_ext * mask_ext[:, tap_time].astype(jnp.bfloat16)[:, None, None, None]
        kernel = jnp.transpose(weight[tap_time][::-1, ::-1], (0, 1, 3, 2))
        spread = lax.conv_general_dilated(
            masked,
            kernel,
            (1, 1),
            ((2, 0), (2, 2)),
            lhs_dilation=(2, 2),
            dimension_numbers=("NHWC", "HWIO", "NHWC"),
            preferred_element_type=jnp.float32,
        )
        pieces.append(spread[:, 1:, 1:])
    even_frames = pieces[2][:-1] + pieces[0][1:]
    odd_frames = pieces[1][1:]
    merged = jnp.stack([even_frames, odd_frames], axis=1)
    return merged.reshape((2 * even_frames.shape[0],) + even_frames.shape[1:])


def positions(counts_row, frame_index):
    starts = jnp.cumsum(counts_row) - counts_row
    latest = jnp.max(jnp.where(starts[None, :] <= frame_index[:, None], starts[None, :], 0), axis=1)
    return frame_index - latest


def tap_masks(place):
    return (place[:, None] >= (2 - jnp.arange(3, dtype=jnp.int32))[None, :]).astype(jnp.float32)


def body(clips, frame_counts, conv_first, conv_down, out_cotangent):
    frames_dev = clips.shape[1]
    rows_dev = clips.shape[2]
    columns_all = clips.shape[3]
    down_frames = frames_dev // 2
    counts_row = frame_counts[0]
    first_frame = lax.axis_index("tm") * frames_dev
    frame_index = first_frame + jnp.arange(frames_dev, dtype=jnp.int32)
    first_mask = tap_masks(positions(counts_row, frame_index))
    down_index = first_frame + 2 * jnp.arange(down_frames + 1, dtype=jnp.int32)
    mask_ext = tap_masks(positions(counts_row, down_index))
    down_mask = mask_ext[:down_frames]
    cells = clips[0]
    scale = 1.0 / math.sqrt(
        lax.axis_size("dp")
        * clips.shape[0]
        * down_frames
        * lax.axis_size("tm")
        * (rows_dev // 2)
        * lax.axis_size("height")
        * (columns_all // 2)
    )
    grads = (out_cotangent[0].astype(jnp.float32) * scale).astype(jnp.bfloat16)
    head, grads_head = cells[:, :1], grads[:, 0:1]
    joined = shifted(jnp.concatenate([head.reshape(-1), grads_head.reshape(-1)]), "height", -1)
    below_cells = joined[: head.size].reshape(head.shape)
    below = joined[head.size :].reshape(grads_head.shape)
    above_cells = shifted(cells[:, rows_dev - 1 :], "height", 1)
    with_rows = jnp.concatenate([above_cells, cells, below_cells], axis=1)
    earlier = shifted(with_rows, "tm", 1)
    input_ext = jnp.concatenate([earlier, with_rows], axis=0)
    pre_act = conv_layer(input_ext, conv_first, first_mask, frames_dev, 1, (1, 1))
    hidden = jax.nn.silu(pre_act).astype(jnp.bfloat16)
    above = shifted(hidden[:, rows_dev - 1 :], "height", 1)
    hidden_rows = jnp.concatenate([above, hidden], axis=1)
    hidden_past = shifted(hidden_rows, "tm", 1)
    hidden_ext = jnp.concatenate([hidden_past, hidden_rows], axis=0)
    encoded = conv_layer(hidden_ext, conv_down, down_mask, down_frames, 2, (1, 0)).astype(
        jnp.bfloat16
    )
    down_local = weight_grad(hidden_ext, grads, down_mask, 2, (1, 0))
    grads_rows = jnp.concatenate([grads, below], axis=1)
    grads_next = shifted(grads_rows, "tm", -1)
    grads_ext = jnp.concatenate([grads_rows, grads_next], axis=0)
    back_hidden = hidden_grad(grads_ext, conv_down, mask_ext).astype(jnp.bfloat16)
    sigma = jax.nn.sigmoid(pre_act)
    pre_grad = (back_hidden.astype(jnp.float32) * sigma * (1.0 + pre_act * (1.0 - sigma))).astype(
        jnp.bfloat16
    )
    first_local = weight_grad(input_ext, pre_grad, first_mask, 1, (1, 1))
    share = conv_first.shape[3] // lax.axis_size("dp")
    quarters = lax.axis_size("dp")

    lanes = conv_first.shape[-1]
    rows_total = 27 * share
    chunks = lax.axis_size("height") // 2
    chunk_rows = -(-rows_total // (chunks * 16)) * 16
    padded_rows = chunk_rows * chunks

    def by_quarter(term):
        term = term.reshape(27, quarters, share, lanes)
        term = jnp.transpose(term, (1, 0, 2, 3)).reshape(quarters, rows_total, lanes)
        return jnp.pad(term, ((0, 0), (0, padded_rows - rows_total), (0, 0)))

    stacked = jnp.stack([by_quarter(first_local), by_quarter(down_local)], axis=1)
    gathered = reduce_gradients(stacked).reshape(2, padded_rows, lanes)[:, :rows_total]
    kernel_shape = (3, 3, 3, share, lanes)
    summed_first = gathered[0].reshape(kernel_shape)
    summed_down = gathered[1].reshape(kernel_shape)
    return (encoded[None], summed_first, summed_down)


def swap(value, axis, bit):
    return lax.ppermute(value, axis, [(i, i ^ bit) for i in range(lax.axis_size(axis))])


def ring_mask(bit, low_bits):
    return bit if bit in low_bits else bit | bit // 2


def swap_rows(value, bits, low_bits):
    count = lax.axis_size("height")
    pairs = []
    for group in range(lax.axis_size("dp")):
        mask = ring_mask(bits[group % 2], low_bits)
        pairs += [(group * count + i, group * count + (i ^ mask)) for i in range(count)]
    return lax.ppermute(value, ("dp", "height"), pairs)


def kept_bit(row, bit, low_bits):
    if bit in low_bits:
        return ((row // bit) ^ (row // (2 * bit))) % 2
    return (row // bit) % 2


def bits_of(count):
    return [1 << k for k in range(count.bit_length() - 1)]


def split_bit(blocks, names, name, high):
    place = names.index(name)
    mine = lax.dynamic_index_in_dim(blocks, high, place, keepdims=False)
    other = lax.dynamic_index_in_dim(blocks, 1 - high, place, keepdims=False)
    return mine, other, names[:place] + names[place + 1 :]


def reduce_gradients(stacked):
    dp_bits = bits_of(lax.axis_size("dp"))
    row_bits = bits_of(lax.axis_size("height"))
    frame_bits = bits_of(lax.axis_size("tm"))
    names = [("dp", bit) for bit in reversed(dp_bits)] + [("height", bit) for bit in reversed(row_bits)]
    blocks = stacked.reshape((2,) * len(names) + (-1, 128))
    for bit in dp_bits[:-1]:
        high = (lax.axis_index("dp") // bit) % 2
        mine, other, names = split_bit(blocks, names, ("dp", bit), high)
        blocks = mine + swap(other, "dp", bit)
    near = row_bits[0::2] + row_bits[1::2]
    crossed = [near[k ^ 1] if (k ^ 1) < len(near) else near[k] for k in range(len(near))]
    stages = list(zip(near, crossed))
    core = lax.axis_index("dp") % 2
    row = lax.axis_index("height")
    held = [names, names]
    low_bits = row_bits[0::2]
    for bits in stages:
        parts = []
        for variant in (0, 1):
            high = kept_bit(row, bits[variant], low_bits)
            mine, other, held[variant] = split_bit(blocks, held[variant], ("height", bits[variant]), high)
            parts.append((mine, other))
        mine = jnp.where(core == 0, parts[0][0], parts[1][0])
        other = jnp.where(core == 0, parts[0][1], parts[1][1])
        blocks = mine + swap_rows(other, bits, low_bits)
    far = dp_bits[-1]
    high = (lax.axis_index("dp") // far) % 2
    mine, other, _ = split_bit(blocks, held[0], ("dp", far), high)
    blocks = mine + swap(other, "dp", far)
    for bit in frame_bits:
        blocks = blocks + swap(blocks, "tm", bit)
    piece = blocks.astype(jnp.bfloat16)
    gathered = lax.all_gather(piece, "height", axis=0, tiled=False)
    owner = [h ^ sum((h >> 1) & bit for bit in low_bits) for h in range(gathered.shape[0])]
    return gathered[np.array(owner)]


def solution(mesh):
    in_specs = (
        P("dp", "tm", "height", None, None),
        P("dp", None),
        P(),
        P(),
        P("dp", "tm", "height", None, None),
    )
    out_specs = (
        P("dp", "tm", "height", None, None),
        P(None, None, None, "dp", None),
        P(None, None, None, "dp", None),
    )
    return jax.shard_map(body, mesh=mesh, in_specs=in_specs, out_specs=out_specs, check_vma=False)
```

```python
import math

import jax
import numpy as np
import jax.numpy as jnp
from jax import lax
from jax.sharding import PartitionSpec as P


def padded_2(cells, sides, width):
    for axis, dim in sides:
        count = lax.axis_size(axis)
        ends = count - 1
        head = lax.slice_in_dim(cells, 0, width, axis=dim)
        tail = lax.slice_in_dim(cells, cells.shape[dim] - width, cells.shape[dim], axis=dim)
        cells = jnp.concatenate(
            [
                lax.ppermute(tail, axis, [(i, (i + 1) % count) for i in range(ends)]),
                cells,
                lax.ppermute(head, axis, [((i + 1) % count, i) for i in range(ends)]),
            ],
            axis=dim,
        )
    return cells


def shifted(value, axis, steps):
    count = lax.axis_size(axis)
    leading, last = (max(0, -steps), min(count, count - steps))
    return lax.ppermute(value, axis, [(source, source + steps) for source in range(leading, last)])


def conv_layer(extended, weight, tap_mask, out_frames, stride, pad_cols):
    summed = None
    for tap_time in range(3):
        frame_slab = extended[tap_time : tap_time + stride * (out_frames - 1) + 1 : stride]
        tap_term = lax.conv_general_dilated(
            frame_slab,
            weight[tap_time],
            (stride, stride),
            ((0, 0), pad_cols),
            dimension_numbers=("NHWC", "HWIO", "NHWC"),
            preferred_element_type=jnp.float32,
        )
        tap_term = tap_term * tap_mask[:, tap_time][:, None, None, None]
        summed = tap_term if summed is None else summed + tap_term
    return summed


def weight_grad(extended, grads, tap_mask, stride, pad_cols):
    out_frames = grads.shape[0]
    blocks = []
    for tap_time in range(3):
        frame_slab = extended[tap_time : tap_time + stride * (out_frames - 1) + 1 : stride]
        masked = grads * tap_mask[:, tap_time].astype(jnp.bfloat16)[:, None, None, None]
        blocks.append(
            lax.conv_general_dilated(
                frame_slab,
                masked,
                (1, 1),
                ((0, 0), pad_cols),
                rhs_dilation=(stride, stride),
                dimension_numbers=("CHWN", "IHWO", "HWNC"),
                preferred_element_type=jnp.float32,
            )
        )
    return jnp.stack(blocks)


def hidden_grad(grads_ext, weight, mask_ext):
    pieces = []
    for tap_time in range(3):
        masked = grads_ext * mask_ext[:, tap_time].astype(jnp.bfloat16)[:, None, None, None]
        kernel = jnp.transpose(weight[tap_time][::-1, ::-1], (0, 1, 3, 2))
        spread = lax.conv_general_dilated(
            masked,
            kernel,
            (1, 1),
            ((2, 0), (2, 2)),
            lhs_dilation=(2, 2),
            dimension_numbers=("NHWC", "HWIO", "NHWC"),
            preferred_element_type=jnp.float32,
        )
        pieces.append(spread[:, 1:, 1:])
    even_frames = pieces[2][:-1] + pieces[0][1:]
    odd_frames = pieces[1][1:]
    merged = jnp.stack([even_frames, odd_frames], axis=1)
    return merged.reshape((2 * even_frames.shape[0],) + even_frames.shape[1:])


def positions(counts_row, frame_index):
    starts = jnp.cumsum(counts_row) - counts_row
    latest = jnp.max(jnp.where(starts[None, :] <= frame_index[:, None], starts[None, :], 0), axis=1)
    return frame_index - latest


def tap_masks(place):
    return (place[:, None] >= (2 - jnp.arange(3, dtype=jnp.int32))[None, :]).astype(jnp.float32)


def body(clips, frame_counts, conv_first, conv_down, out_cotangent):
    frames_dev = clips.shape[1]
    rows_dev = clips.shape[2]
    columns_all = clips.shape[3]
    down_frames = frames_dev // 2
    counts_row = frame_counts[0]
    first_frame = lax.axis_index("tm") * frames_dev
    frame_index = first_frame + jnp.arange(frames_dev, dtype=jnp.int32)
    first_mask = tap_masks(positions(counts_row, frame_index))
    down_index = first_frame + 2 * jnp.arange(down_frames + 1, dtype=jnp.int32)
    mask_ext = tap_masks(positions(counts_row, down_index))
    down_mask = mask_ext[:down_frames]
    cells = clips[0]
    scale = 1.0 / math.sqrt(
        lax.axis_size("dp")
        * clips.shape[0]
        * down_frames
        * lax.axis_size("tm")
        * (rows_dev // 2)
        * lax.axis_size("height")
        * (columns_all // 2)
    )
    grads = (out_cotangent[0].astype(jnp.float32) * scale).astype(jnp.bfloat16)
    head, grads_head = cells[:, :1], grads[:, 0:1]
    joined = shifted(jnp.concatenate([head.reshape(-1), grads_head.reshape(-1)]), "height", -1)
    below_cells = joined[: head.size].reshape(head.shape)
    below = joined[head.size :].reshape(grads_head.shape)
    above_cells = shifted(cells[:, rows_dev - 2 :], "height", 1)
    with_rows = jnp.concatenate([above_cells, cells, below_cells], axis=1)
    earlier = shifted(with_rows, "tm", 1)
    wide_ext = jnp.concatenate([earlier, with_rows], axis=0)
    wide_pre = conv_layer(wide_ext, conv_first, first_mask, frames_dev, 1, (1, 1))
    row_valid = jnp.arange(rows_dev + 1) >= jnp.where(lax.axis_index("height") == 0, 1, 0)
    hidden_rows = jnp.where(
        row_valid[None, :, None, None], jax.nn.silu(wide_pre).astype(jnp.bfloat16), 0
    ).astype(jnp.bfloat16)
    pre_act = wide_pre[:, 1:]
    input_ext = wide_ext[:, 1:]
    hidden_past = shifted(hidden_rows, "tm", 1)
    hidden_ext = jnp.concatenate([hidden_past, hidden_rows], axis=0)
    encoded = conv_layer(hidden_ext, conv_down, down_mask, down_frames, 2, (1, 0)).astype(
        jnp.bfloat16
    )
    down_local = weight_grad(hidden_ext, grads, down_mask, 2, (1, 0))
    grads_rows = jnp.concatenate([grads, below], axis=1)
    grads_next = shifted(grads_rows, "tm", -1)
    grads_ext = jnp.concatenate([grads_rows, grads_next], axis=0)
    back_hidden = hidden_grad(grads_ext, conv_down, mask_ext).astype(jnp.bfloat16)
    sigma = jax.nn.sigmoid(pre_act)
    pre_grad = (back_hidden.astype(jnp.float32) * sigma * (1.0 + pre_act * (1.0 - sigma))).astype(
        jnp.bfloat16
    )
    first_local = weight_grad(input_ext, pre_grad, first_mask, 1, (1, 1))
    share = conv_first.shape[3] // lax.axis_size("dp")
    quarters = lax.axis_size("dp")

    lanes = conv_first.shape[-1]
    rows_total = 27 * share
    chunks = lax.axis_size("height") // 2
    chunk_rows = -(-rows_total // (chunks * 16)) * 16
    padded_rows = chunk_rows * chunks

    def by_quarter(term):
        term = term.reshape(27, quarters, share, lanes)
        term = jnp.transpose(term, (1, 0, 2, 3)).reshape(quarters, rows_total, lanes)
        return jnp.pad(term, ((0, 0), (0, padded_rows - rows_total), (0, 0)))

    stacked = jnp.stack([by_quarter(first_local), by_quarter(down_local)], axis=1)
    gathered = reduce_gradients(stacked).reshape(2, padded_rows, lanes)[:, :rows_total]
    kernel_shape = (3, 3, 3, share, lanes)
    summed_first = gathered[0].reshape(kernel_shape)
    summed_down = gathered[1].reshape(kernel_shape)
    return (encoded[None], summed_first, summed_down)


def swap(value, axis, bit):
    return lax.ppermute(value, axis, [(i, i ^ bit) for i in range(lax.axis_size(axis))])


def ring_mask(bit, low_bits):
    return bit if bit in low_bits else bit | bit // 2


def swap_rows(value, bits, low_bits):
    count = lax.axis_size("height")
    pairs = []
    for group in range(lax.axis_size("dp")):
        mask = ring_mask(bits[group % 2], low_bits)
        pairs += [(group * count + i, group * count + (i ^ mask)) for i in range(count)]
    return lax.ppermute(value, ("dp", "height"), pairs)


def kept_bit(row, bit, low_bits):
    if bit in low_bits:
        return ((row // bit) ^ (row // (2 * bit))) % 2
    return (row // bit) % 2


def bits_of(count):
    return [1 << k for k in range(count.bit_length() - 1)]


def split_bit(blocks, names, name, high):
    place = names.index(name)
    mine = lax.dynamic_index_in_dim(blocks, high, place, keepdims=False)
    other = lax.dynamic_index_in_dim(blocks, 1 - high, place, keepdims=False)
    return mine, other, names[:place] + names[place + 1 :]


def reduce_gradients(stacked):
    dp_bits = bits_of(lax.axis_size("dp"))
    row_bits = bits_of(lax.axis_size("height"))
    frame_bits = bits_of(lax.axis_size("tm"))
    names = [("dp", bit) for bit in reversed(dp_bits)] + [("height", bit) for bit in reversed(row_bits)]
    blocks = stacked.reshape((2,) * len(names) + (-1, 128))
    for bit in dp_bits[:-1]:
        high = (lax.axis_index("dp") // bit) % 2
        mine, other, names = split_bit(blocks, names, ("dp", bit), high)
        blocks = mine + swap(other, "dp", bit)
    near = row_bits[0::2] + row_bits[1::2]
    crossed = [near[k ^ 1] if (k ^ 1) < len(near) else near[k] for k in range(len(near))]
    stages = list(zip(near, crossed))
    core = lax.axis_index("dp") % 2
    row = lax.axis_index("height")
    held = [names, names]
    low_bits = row_bits[0::2]
    for bits in stages:
        parts = []
        for variant in (0, 1):
            high = kept_bit(row, bits[variant], low_bits)
            mine, other, held[variant] = split_bit(blocks, held[variant], ("height", bits[variant]), high)
            parts.append((mine, other))
        mine = jnp.where(core == 0, parts[0][0], parts[1][0])
        other = jnp.where(core == 0, parts[0][1], parts[1][1])
        blocks = mine + swap_rows(other, bits, low_bits)
    far = dp_bits[-1]
    high = (lax.axis_index("dp") // far) % 2
    mine, other, _ = split_bit(blocks, held[0], ("dp", far), high)
    blocks = mine + swap(other, "dp", far)
    for bit in frame_bits:
        blocks = blocks + swap(blocks, "tm", bit)
    piece = blocks.astype(jnp.bfloat16)
    gathered = lax.all_gather(piece, "height", axis=0, tiled=False)
    owner = [h ^ sum((h >> 1) & bit for bit in low_bits) for h in range(gathered.shape[0])]
    return gathered[np.array(owner)]


def solution(mesh):
    in_specs = (
        P("dp", "tm", "height", None, None),
        P("dp", None),
        P(),
        P(),
        P("dp", "tm", "height", None, None),
    )
    out_specs = (
        P("dp", "tm", "height", None, None),
        P(None, None, None, "dp", None),
        P(None, None, None, "dp", None),
    )
    return jax.shard_map(body, mesh=mesh, in_specs=in_specs, out_specs=out_specs, check_vma=False)
```

```python
import math

import jax
import numpy as np
import jax.numpy as jnp
from jax import lax
from jax.sharding import PartitionSpec as P


def padded_2(cells, sides, width):
    for axis, dim in sides:
        count = lax.axis_size(axis)
        ends = count - 1
        head = lax.slice_in_dim(cells, 0, width, axis=dim)
        tail = lax.slice_in_dim(cells, cells.shape[dim] - width, cells.shape[dim], axis=dim)
        cells = jnp.concatenate(
            [
                lax.ppermute(tail, axis, [(i, (i + 1) % count) for i in range(ends)]),
                cells,
                lax.ppermute(head, axis, [((i + 1) % count, i) for i in range(ends)]),
            ],
            axis=dim,
        )
    return cells


def shifted(value, axis, steps):
    count = lax.axis_size(axis)
    leading, last = (max(0, -steps), min(count, count - steps))
    return lax.ppermute(value, axis, [(source, source + steps) for source in range(leading, last)])


def conv_layer(extended, weight, tap_mask, out_frames, stride, pad_cols):
    summed = None
    for tap_time in range(3):
        frame_slab = extended[tap_time : tap_time + stride * (out_frames - 1) + 1 : stride]
        tap_term = lax.conv_general_dilated(
            frame_slab,
            weight[tap_time],
            (stride, stride),
            ((0, 0), pad_cols),
            dimension_numbers=("NHWC", "HWIO", "NHWC"),
            preferred_element_type=jnp.float32,
        )
        tap_term = tap_term * tap_mask[:, tap_time][:, None, None, None]
        summed = tap_term if summed is None else summed + tap_term
    return summed


def weight_grad(extended, grads, tap_mask, stride, pad_cols):
    out_frames = grads.shape[0]
    blocks = []
    for tap_time in range(3):
        frame_slab = extended[tap_time : tap_time + stride * (out_frames - 1) + 1 : stride]
        masked = grads * tap_mask[:, tap_time].astype(jnp.bfloat16)[:, None, None, None]
        blocks.append(
            lax.conv_general_dilated(
                frame_slab,
                masked,
                (1, 1),
                ((0, 0), pad_cols),
                rhs_dilation=(stride, stride),
                dimension_numbers=("CHWN", "IHWO", "HWNC"),
                preferred_element_type=jnp.float32,
            )
        )
    return jnp.stack(blocks)


def hidden_grad(grads_ext, weight, mask_ext):
    pieces = []
    for tap_time in range(3):
        masked = grads_ext * mask_ext[:, tap_time].astype(jnp.bfloat16)[:, None, None, None]
        kernel = jnp.transpose(weight[tap_time][::-1, ::-1], (0, 1, 3, 2))
        spread = lax.conv_general_dilated(
            masked,
            kernel,
            (1, 1),
            ((2, 0), (2, 2)),
            lhs_dilation=(2, 2),
            dimension_numbers=("NHWC", "HWIO", "NHWC"),
            preferred_element_type=jnp.float32,
        )
        pieces.append(spread[:, 1:, 1:])
    even_frames = pieces[2][:-1] + pieces[0][1:]
    odd_frames = pieces[1][1:]
    merged = jnp.stack([even_frames, odd_frames], axis=1)
    return merged.reshape((2 * even_frames.shape[0],) + even_frames.shape[1:])


def positions(counts_row, frame_index):
    starts = jnp.cumsum(counts_row) - counts_row
    latest = jnp.max(jnp.where(starts[None, :] <= frame_index[:, None], starts[None, :], 0), axis=1)
    return frame_index - latest


def tap_masks(place):
    return (place[:, None] >= (2 - jnp.arange(3, dtype=jnp.int32))[None, :]).astype(jnp.float32)


def body(clips, frame_counts, conv_first, conv_down, out_cotangent):
    frames_dev = clips.shape[1]
    rows_dev = clips.shape[2]
    columns_all = clips.shape[3]
    down_frames = frames_dev // 2
    counts_row = frame_counts[0]
    first_frame = lax.axis_index("tm") * frames_dev
    frame_index = first_frame + jnp.arange(frames_dev, dtype=jnp.int32)
    first_mask = tap_masks(positions(counts_row, frame_index))
    down_index = first_frame + 2 * jnp.arange(down_frames + 1, dtype=jnp.int32)
    mask_ext = tap_masks(positions(counts_row, down_index))
    down_mask = mask_ext[:down_frames]
    cells = clips[0]
    scale = 1.0 / math.sqrt(
        lax.axis_size("dp")
        * clips.shape[0]
        * down_frames
        * lax.axis_size("tm")
        * (rows_dev // 2)
        * lax.axis_size("height")
        * (columns_all // 2)
    )
    grads = (out_cotangent[0].astype(jnp.float32) * scale).astype(jnp.bfloat16)
    head, grads_head = cells[:, :1], grads[:, 0:1]
    joined = shifted(jnp.concatenate([head.reshape(-1), grads_head.reshape(-1)]), "height", -1)
    below_cells = joined[: head.size].reshape(head.shape)
    below = joined[head.size :].reshape(grads_head.shape)
    above_cells = shifted(cells[:, rows_dev - 1 :], "height", 1)
    with_rows = jnp.concatenate([above_cells, cells, below_cells], axis=1)
    earlier = shifted(with_rows, "tm", 1)
    input_ext = jnp.concatenate([earlier, with_rows], axis=0)
    pre_act = conv_layer(input_ext, conv_first, first_mask, frames_dev, 1, (1, 1))
    hidden = jax.nn.silu(pre_act).astype(jnp.bfloat16)
    above = shifted(hidden[:, rows_dev - 1 :], "height", 1)
    hidden_rows = jnp.concatenate([above, hidden], axis=1)
    hidden_past = shifted(hidden_rows, "tm", 1)
    grads_rows = jnp.concatenate([grads, below], axis=1)
    grads_next = shifted(grads_rows, "tm", -1)
    grads_ext = jnp.concatenate([grads_rows, grads_next], axis=0)
    back_hidden = hidden_grad(grads_ext, conv_down, mask_ext).astype(jnp.bfloat16)
    sigma = jax.nn.sigmoid(pre_act)
    pre_grad = (back_hidden.astype(jnp.float32) * sigma * (1.0 + pre_act * (1.0 - sigma))).astype(
        jnp.bfloat16
    )
    first_local = weight_grad(input_ext, pre_grad, first_mask, 1, (1, 1))
    hidden_past, first_local = lax.optimization_barrier((hidden_past, first_local))
    hidden_ext = jnp.concatenate([hidden_past, hidden_rows], axis=0)
    encoded = conv_layer(hidden_ext, conv_down, down_mask, down_frames, 2, (1, 0)).astype(
        jnp.bfloat16
    )
    down_local = weight_grad(hidden_ext, grads, down_mask, 2, (1, 0))
    share = conv_first.shape[3] // lax.axis_size("dp")
    quarters = lax.axis_size("dp")

    lanes = conv_first.shape[-1]
    rows_total = 27 * share
    chunks = lax.axis_size("height") // 2
    chunk_rows = -(-rows_total // (chunks * 16)) * 16
    padded_rows = chunk_rows * chunks

    def by_quarter(term):
        term = term.reshape(27, quarters, share, lanes)
        term = jnp.transpose(term, (1, 0, 2, 3)).reshape(quarters, rows_total, lanes)
        return jnp.pad(term, ((0, 0), (0, padded_rows - rows_total), (0, 0)))

    stacked = jnp.stack([by_quarter(first_local), by_quarter(down_local)], axis=1)
    gathered = reduce_gradients(stacked).reshape(2, padded_rows, lanes)[:, :rows_total]
    kernel_shape = (3, 3, 3, share, lanes)
    summed_first = gathered[0].reshape(kernel_shape)
    summed_down = gathered[1].reshape(kernel_shape)
    return (encoded[None], summed_first, summed_down)


def swap(value, axis, bit):
    return lax.ppermute(value, axis, [(i, i ^ bit) for i in range(lax.axis_size(axis))])


def ring_mask(bit, low_bits):
    return bit if bit in low_bits else bit | bit // 2


def swap_rows(value, bits, low_bits):
    count = lax.axis_size("height")
    pairs = []
    for group in range(lax.axis_size("dp")):
        mask = ring_mask(bits[group % 2], low_bits)
        pairs += [(group * count + i, group * count + (i ^ mask)) for i in range(count)]
    return lax.ppermute(value, ("dp", "height"), pairs)


def kept_bit(row, bit, low_bits):
    if bit in low_bits:
        return ((row // bit) ^ (row // (2 * bit))) % 2
    return (row // bit) % 2


def bits_of(count):
    return [1 << k for k in range(count.bit_length() - 1)]


def split_bit(blocks, names, name, high):
    place = names.index(name)
    mine = lax.dynamic_index_in_dim(blocks, high, place, keepdims=False)
    other = lax.dynamic_index_in_dim(blocks, 1 - high, place, keepdims=False)
    return mine, other, names[:place] + names[place + 1 :]


def reduce_gradients(stacked):
    dp_bits = bits_of(lax.axis_size("dp"))
    row_bits = bits_of(lax.axis_size("height"))
    frame_bits = bits_of(lax.axis_size("tm"))
    names = [("dp", bit) for bit in reversed(dp_bits)] + [("height", bit) for bit in reversed(row_bits)]
    blocks = stacked.reshape((2,) * len(names) + (-1, 128))
    for bit in dp_bits[:-1]:
        high = (lax.axis_index("dp") // bit) % 2
        mine, other, names = split_bit(blocks, names, ("dp", bit), high)
        blocks = mine + swap(other, "dp", bit)
    near = row_bits[0::2] + row_bits[1::2]
    crossed = [near[k ^ 1] if (k ^ 1) < len(near) else near[k] for k in range(len(near))]
    stages = list(zip(near, crossed))
    core = lax.axis_index("dp") % 2
    row = lax.axis_index("height")
    held = [names, names]
    low_bits = row_bits[0::2]
    for bits in stages:
        parts = []
        for variant in (0, 1):
            high = kept_bit(row, bits[variant], low_bits)
            mine, other, held[variant] = split_bit(blocks, held[variant], ("height", bits[variant]), high)
            parts.append((mine, other))
        mine = jnp.where(core == 0, parts[0][0], parts[1][0])
        other = jnp.where(core == 0, parts[0][1], parts[1][1])
        blocks = mine + swap_rows(other, bits, low_bits)
    far = dp_bits[-1]
    high = (lax.axis_index("dp") // far) % 2
    mine, other, _ = split_bit(blocks, held[0], ("dp", far), high)
    blocks = mine + swap(other, "dp", far)
    for bit in frame_bits:
        blocks = blocks + swap(blocks, "tm", bit)
    piece = blocks.astype(jnp.bfloat16)
    gathered = lax.all_gather(piece, "height", axis=0, tiled=False)
    owner = [h ^ sum((h >> 1) & bit for bit in low_bits) for h in range(gathered.shape[0])]
    return gathered[np.array(owner)]


def solution(mesh):
    in_specs = (
        P("dp", "tm", "height", None, None),
        P("dp", None),
        P(),
        P(),
        P("dp", "tm", "height", None, None),
    )
    out_specs = (
        P("dp", "tm", "height", None, None),
        P(None, None, None, "dp", None),
        P(None, None, None, "dp", None),
    )
    return jax.shard_map(body, mesh=mesh, in_specs=in_specs, out_specs=out_specs, check_vma=False)
```

```python
import math

import jax
import numpy as np
import jax.numpy as jnp
from jax import lax
from jax.sharding import PartitionSpec as P


def padded_2(cells, sides, width):
    for axis, dim in sides:
        count = lax.axis_size(axis)
        ends = count - 1
        head = lax.slice_in_dim(cells, 0, width, axis=dim)
        tail = lax.slice_in_dim(cells, cells.shape[dim] - width, cells.shape[dim], axis=dim)
        cells = jnp.concatenate(
            [
                lax.ppermute(tail, axis, [(i, (i + 1) % count) for i in range(ends)]),
                cells,
                lax.ppermute(head, axis, [((i + 1) % count, i) for i in range(ends)]),
            ],
            axis=dim,
        )
    return cells


def shifted(value, axis, steps):
    count = lax.axis_size(axis)
    leading, last = (max(0, -steps), min(count, count - steps))
    return lax.ppermute(value, axis, [(source, source + steps) for source in range(leading, last)])


def conv_layer(extended, weight, tap_mask, out_frames, stride, pad_cols):
    summed = None
    for tap_time in range(3):
        frame_slab = extended[tap_time : tap_time + stride * (out_frames - 1) + 1 : stride]
        tap_term = lax.conv_general_dilated(
            frame_slab,
            weight[tap_time],
            (stride, stride),
            ((0, 0), pad_cols),
            dimension_numbers=("NHWC", "HWIO", "NHWC"),
            preferred_element_type=jnp.float32,
        )
        tap_term = tap_term * tap_mask[:, tap_time][:, None, None, None]
        summed = tap_term if summed is None else summed + tap_term
    return summed


def weight_grad(extended, grads, tap_mask, stride, pad_cols):
    out_frames = grads.shape[0]
    blocks = []
    for tap_time in range(3):
        frame_slab = extended[tap_time : tap_time + stride * (out_frames - 1) + 1 : stride]
        masked = grads * tap_mask[:, tap_time].astype(jnp.bfloat16)[:, None, None, None]
        blocks.append(
            lax.conv_general_dilated(
                frame_slab,
                masked,
                (1, 1),
                ((0, 0), pad_cols),
                rhs_dilation=(stride, stride),
                dimension_numbers=("CHWN", "IHWO", "HWNC"),
                preferred_element_type=jnp.float32,
            )
        )
    return jnp.stack(blocks)


def hidden_grad(grads_ext, weight, mask_ext):
    pieces = []
    for tap_time in range(3):
        masked = grads_ext * mask_ext[:, tap_time].astype(jnp.bfloat16)[:, None, None, None]
        kernel = jnp.transpose(weight[tap_time][::-1, ::-1], (0, 1, 3, 2))
        spread = lax.conv_general_dilated(
            masked,
            kernel,
            (1, 1),
            ((2, 0), (2, 2)),
            lhs_dilation=(2, 2),
            dimension_numbers=("NHWC", "HWIO", "NHWC"),
            preferred_element_type=jnp.float32,
        )
        pieces.append(spread[:, 1:, 1:])
    even_frames = pieces[2][:-1] + pieces[0][1:]
    odd_frames = pieces[1][1:]
    merged = jnp.stack([even_frames, odd_frames], axis=1)
    return merged.reshape((2 * even_frames.shape[0],) + even_frames.shape[1:])


def positions(counts_row, frame_index):
    starts = jnp.cumsum(counts_row) - counts_row
    latest = jnp.max(jnp.where(starts[None, :] <= frame_index[:, None], starts[None, :], 0), axis=1)
    return frame_index - latest


def tap_masks(place):
    return (place[:, None] >= (2 - jnp.arange(3, dtype=jnp.int32))[None, :]).astype(jnp.float32)


def body(clips, frame_counts, conv_first, conv_down, out_cotangent):
    frames_dev = clips.shape[1]
    rows_dev = clips.shape[2]
    columns_all = clips.shape[3]
    down_frames = frames_dev // 2
    counts_row = frame_counts[0]
    first_frame = lax.axis_index("tm") * frames_dev
    frame_index = first_frame + jnp.arange(frames_dev, dtype=jnp.int32)
    first_mask = tap_masks(positions(counts_row, frame_index))
    down_index = first_frame + 2 * jnp.arange(down_frames + 1, dtype=jnp.int32)
    mask_ext = tap_masks(positions(counts_row, down_index))
    down_mask = mask_ext[:down_frames]
    cells = clips[0]
    scale = 1.0 / math.sqrt(
        lax.axis_size("dp")
        * clips.shape[0]
        * down_frames
        * lax.axis_size("tm")
        * (rows_dev // 2)
        * lax.axis_size("height")
        * (columns_all // 2)
    )
    grads = (out_cotangent[0].astype(jnp.float32) * scale).astype(jnp.bfloat16)
    head, grads_head = cells[:, :1], grads[:, 0:1]
    joined = shifted(jnp.concatenate([head.reshape(-1), grads_head.reshape(-1)]), "height", -1)
    below_cells = joined[: head.size].reshape(head.shape)
    below = joined[head.size :].reshape(grads_head.shape)
    above_cells = shifted(cells[:, rows_dev - 1 :], "height", 1)
    with_rows = jnp.concatenate([above_cells, cells, below_cells], axis=1)
    earlier = shifted(with_rows, "tm", 1)
    input_ext = jnp.concatenate([earlier, with_rows], axis=0)
    pre_act = conv_layer(input_ext, conv_first, first_mask, frames_dev, 1, (1, 1))
    hidden = jax.nn.silu(pre_act).astype(jnp.bfloat16)
    above = shifted(hidden[:, rows_dev - 1 :], "height", 1)
    hidden_rows = jnp.concatenate([above, hidden], axis=1)
    hidden_past = shifted(hidden_rows, "tm", 1)
    grads_rows = jnp.concatenate([grads, below], axis=1)
    grads_next = shifted(grads_rows, "tm", -1)
    grads_ext = jnp.concatenate([grads_rows, grads_next], axis=0)
    back_hidden = hidden_grad(grads_ext, conv_down, mask_ext).astype(jnp.bfloat16)
    sigma = jax.nn.sigmoid(pre_act)
    pre_grad = (back_hidden.astype(jnp.float32) * sigma * (1.0 + pre_act * (1.0 - sigma))).astype(
        jnp.bfloat16
    )
    first_local = weight_grad(input_ext, pre_grad, first_mask, 1, (1, 1))
    hidden_past, first_local = lax.optimization_barrier((hidden_past, first_local))
    hidden_ext = jnp.concatenate([hidden_past, hidden_rows], axis=0)
    encoded = conv_layer(hidden_ext, conv_down, down_mask, down_frames, 2, (1, 0)).astype(
        jnp.bfloat16
    )
    down_local = weight_grad(hidden_ext, grads, down_mask, 2, (1, 0))
    share = conv_first.shape[3] // lax.axis_size("dp")
    quarters = lax.axis_size("dp")

    lanes = conv_first.shape[-1]
    rows_total = 27 * share
    chunks = lax.axis_size("height") // 2
    chunk_rows = -(-rows_total // (chunks * 16)) * 16
    padded_rows = chunk_rows * chunks

    def by_quarter(term):
        term = term.reshape(27, quarters, share, lanes)
        term = jnp.transpose(term, (1, 0, 2, 3)).reshape(quarters, rows_total, lanes)
        return jnp.pad(term, ((0, 0), (0, padded_rows - rows_total), (0, 0)))

    stacked = jnp.stack([by_quarter(first_local), by_quarter(down_local)], axis=1)
    gathered = reduce_gradients(stacked).reshape(2, padded_rows, lanes)[:, :rows_total]
    kernel_shape = (3, 3, 3, share, lanes)
    summed_first = gathered[0].reshape(kernel_shape)
    summed_down = gathered[1].reshape(kernel_shape)
    return (encoded[None], summed_first, summed_down)


def swap(value, axis, bit):
    return lax.ppermute(value, axis, [(i, i ^ bit) for i in range(lax.axis_size(axis))])


def ring_mask(bit, low_bits):
    return bit if bit in low_bits else bit | bit // 2


def swap_rows(value, bits, low_bits):
    count = lax.axis_size("height")
    pairs = []
    for group in range(lax.axis_size("dp")):
        mask = ring_mask(bits[group % 2], low_bits)
        pairs += [(group * count + i, group * count + (i ^ mask)) for i in range(count)]
    return lax.ppermute(value, ("dp", "height"), pairs)


def kept_bit(row, bit, low_bits):
    if bit in low_bits:
        return ((row // bit) ^ (row // (2 * bit))) % 2
    return (row // bit) % 2


def bits_of(count):
    return [1 << k for k in range(count.bit_length() - 1)]


def split_bit(blocks, names, name, high):
    place = names.index(name)
    mine = lax.dynamic_index_in_dim(blocks, high, place, keepdims=False)
    other = lax.dynamic_index_in_dim(blocks, 1 - high, place, keepdims=False)
    return mine, other, names[:place] + names[place + 1 :]


def reduce_gradients(stacked):
    dp_bits = bits_of(lax.axis_size("dp"))
    row_bits = bits_of(lax.axis_size("height"))
    frame_bits = bits_of(lax.axis_size("tm"))
    names = [("dp", bit) for bit in reversed(dp_bits)] + [("height", bit) for bit in reversed(row_bits)]
    blocks = stacked.reshape((2,) * len(names) + (-1, 128))
    for bit in dp_bits[:-1]:
        high = (lax.axis_index("dp") // bit) % 2
        mine, other, names = split_bit(blocks, names, ("dp", bit), high)
        blocks = mine + swap(other, "dp", bit)
    near = row_bits[0::2] + row_bits[1::2]
    crossed = [near[k ^ 1] if (k ^ 1) < len(near) else near[k] for k in range(len(near))]
    stages = list(zip(near, crossed))
    core = lax.axis_index("dp") % 2
    row = lax.axis_index("height")
    held = [names, names]
    low_bits = row_bits[0::2]
    for bits in stages:
        parts = []
        for variant in (0, 1):
            high = kept_bit(row, bits[variant], low_bits)
            mine, other, held[variant] = split_bit(blocks, held[variant], ("height", bits[variant]), high)
            parts.append((mine, other))
        mine = jnp.where(core == 0, parts[0][0], parts[1][0])
        other = jnp.where(core == 0, parts[0][1], parts[1][1])
        blocks = mine + swap_rows(other, bits, low_bits)
    for bit in frame_bits[:-1]:
        blocks = blocks + swap(blocks, "tm", bit)
    far, top = dp_bits[-1], frame_bits[-1]
    frames = lax.axis_size("tm")
    high = (lax.axis_index("dp") // far) % 2
    mine, other, _ = split_bit(blocks, held[0], ("dp", far), high)

    def send(value, group_flip, frame_flip):
        pairs = [
            (group * frames + t, (group ^ group_flip) * frames + (t ^ frame_flip))
            for group in range(lax.axis_size("dp"))
            for t in range(frames)
        ]
        return lax.ppermute(value, ("dp", "tm"), pairs)

    total = mine + send(mine, 0, top) + send(other, far, 0) + send(other, far, top)
    piece = total.astype(jnp.bfloat16)
    gathered = lax.all_gather(piece, "height", axis=0, tiled=False)
    owner = [h ^ sum((h >> 1) & bit for bit in low_bits) for h in range(gathered.shape[0])]
    return gathered[np.array(owner)]


def solution(mesh):
    in_specs = (
        P("dp", "tm", "height", None, None),
        P("dp", None),
        P(),
        P(),
        P("dp", "tm", "height", None, None),
    )
    out_specs = (
        P("dp", "tm", "height", None, None),
        P(None, None, None, "dp", None),
        P(None, None, None, "dp", None),
    )
    return jax.shard_map(body, mesh=mesh, in_specs=in_specs, out_specs=out_specs, check_vma=False)
```

```python
import math

import jax
import numpy as np
import jax.numpy as jnp
from jax import lax
from jax.sharding import PartitionSpec as P


def padded_2(cells, sides, width):
    for axis, dim in sides:
        count = lax.axis_size(axis)
        ends = count - 1
        head = lax.slice_in_dim(cells, 0, width, axis=dim)
        tail = lax.slice_in_dim(cells, cells.shape[dim] - width, cells.shape[dim], axis=dim)
        cells = jnp.concatenate(
            [
                lax.ppermute(tail, axis, [(i, (i + 1) % count) for i in range(ends)]),
                cells,
                lax.ppermute(head, axis, [((i + 1) % count, i) for i in range(ends)]),
            ],
            axis=dim,
        )
    return cells


def shifted(value, axis, steps):
    count = lax.axis_size(axis)
    leading, last = (max(0, -steps), min(count, count - steps))
    return lax.ppermute(value, axis, [(source, source + steps) for source in range(leading, last)])


def conv_layer(extended, weight, tap_mask, out_frames, stride, pad_cols):
    summed = None
    for tap_time in range(3):
        frame_slab = extended[tap_time : tap_time + stride * (out_frames - 1) + 1 : stride]
        tap_term = lax.conv_general_dilated(
            frame_slab,
            weight[tap_time],
            (stride, stride),
            ((0, 0), pad_cols),
            dimension_numbers=("NHWC", "HWIO", "NHWC"),
            preferred_element_type=jnp.float32,
        )
        tap_term = tap_term * tap_mask[:, tap_time][:, None, None, None]
        summed = tap_term if summed is None else summed + tap_term
    return summed


def weight_grad(extended, grads, tap_mask, stride, pad_cols):
    out_frames = grads.shape[0]
    blocks = []
    for tap_time in range(3):
        frame_slab = extended[tap_time : tap_time + stride * (out_frames - 1) + 1 : stride]
        masked = grads * tap_mask[:, tap_time].astype(jnp.bfloat16)[:, None, None, None]
        blocks.append(
            lax.conv_general_dilated(
                frame_slab,
                masked,
                (1, 1),
                ((0, 0), pad_cols),
                rhs_dilation=(stride, stride),
                dimension_numbers=("CHWN", "IHWO", "HWNC"),
                preferred_element_type=jnp.float32,
            )
        )
    return jnp.stack(blocks)


def hidden_grad(grads_ext, weight, mask_ext):
    pieces = []
    for tap_time in range(3):
        masked = grads_ext * mask_ext[:, tap_time].astype(jnp.bfloat16)[:, None, None, None]
        kernel = jnp.transpose(weight[tap_time][::-1, ::-1], (0, 1, 3, 2))
        spread = lax.conv_general_dilated(
            masked,
            kernel,
            (1, 1),
            ((2, 0), (2, 2)),
            lhs_dilation=(2, 2),
            dimension_numbers=("NHWC", "HWIO", "NHWC"),
            preferred_element_type=jnp.float32,
        )
        pieces.append(spread[:, 1:, 1:])
    even_frames = pieces[2][:-1] + pieces[0][1:]
    odd_frames = pieces[1][1:]
    merged = jnp.stack([even_frames, odd_frames], axis=1)
    return merged.reshape((2 * even_frames.shape[0],) + even_frames.shape[1:])


def positions(counts_row, frame_index):
    starts = jnp.cumsum(counts_row) - counts_row
    latest = jnp.max(jnp.where(starts[None, :] <= frame_index[:, None], starts[None, :], 0), axis=1)
    return frame_index - latest


def tap_masks(place):
    return (place[:, None] >= (2 - jnp.arange(3, dtype=jnp.int32))[None, :]).astype(jnp.float32)


def body(clips, frame_counts, conv_first, conv_down, out_cotangent):
    frames_dev = clips.shape[1]
    rows_dev = clips.shape[2]
    columns_all = clips.shape[3]
    down_frames = frames_dev // 2
    counts_row = frame_counts[0]
    first_frame = lax.axis_index("tm") * frames_dev
    frame_index = first_frame + jnp.arange(frames_dev, dtype=jnp.int32)
    first_mask = tap_masks(positions(counts_row, frame_index))
    down_index = first_frame + 2 * jnp.arange(down_frames + 1, dtype=jnp.int32)
    mask_ext = tap_masks(positions(counts_row, down_index))
    down_mask = mask_ext[:down_frames]
    cells = clips[0]
    scale = 1.0 / math.sqrt(
        lax.axis_size("dp")
        * clips.shape[0]
        * down_frames
        * lax.axis_size("tm")
        * (rows_dev // 2)
        * lax.axis_size("height")
        * (columns_all // 2)
    )
    grads = (out_cotangent[0].astype(jnp.float32) * scale).astype(jnp.bfloat16)
    head, grads_head = cells[:, :1], grads[:, 0:1]
    joined = shifted(jnp.concatenate([head.reshape(-1), grads_head.reshape(-1)]), "height", -1)
    below_cells = joined[: head.size].reshape(head.shape)
    below = joined[head.size :].reshape(grads_head.shape)
    above_cells = shifted(cells[:, rows_dev - 2 :], "height", 1)
    with_rows = jnp.concatenate([above_cells, cells, below_cells], axis=1)
    earlier = shifted(with_rows, "tm", 1)
    wide_ext = jnp.concatenate([earlier, with_rows], axis=0)
    wide_pre = conv_layer(wide_ext, conv_first, first_mask, frames_dev, 1, (1, 1))
    row_valid = jnp.arange(rows_dev + 1) >= jnp.where(lax.axis_index("height") == 0, 1, 0)
    hidden_rows = jnp.where(
        row_valid[None, :, None, None], jax.nn.silu(wide_pre).astype(jnp.bfloat16), 0
    ).astype(jnp.bfloat16)
    pre_act = wide_pre[:, 1:]
    input_ext = wide_ext[:, 1:]
    hidden_past = shifted(hidden_rows, "tm", 1)
    grads_rows = jnp.concatenate([grads, below], axis=1)
    grads_next = shifted(grads_rows, "tm", -1)
    grads_ext = jnp.concatenate([grads_rows, grads_next], axis=0)
    back_hidden = hidden_grad(grads_ext, conv_down, mask_ext).astype(jnp.bfloat16)
    sigma = jax.nn.sigmoid(pre_act)
    pre_grad = (back_hidden.astype(jnp.float32) * sigma * (1.0 + pre_act * (1.0 - sigma))).astype(
        jnp.bfloat16
    )
    first_local = weight_grad(input_ext, pre_grad, first_mask, 1, (1, 1))
    hidden_past, first_local = lax.optimization_barrier((hidden_past, first_local))
    hidden_ext = jnp.concatenate([hidden_past, hidden_rows], axis=0)
    encoded = conv_layer(hidden_ext, conv_down, down_mask, down_frames, 2, (1, 0)).astype(
        jnp.bfloat16
    )
    down_local = weight_grad(hidden_ext, grads, down_mask, 2, (1, 0))
    share = conv_first.shape[3] // lax.axis_size("dp")
    quarters = lax.axis_size("dp")

    lanes = conv_first.shape[-1]
    rows_total = 27 * share
    chunks = lax.axis_size("height") // 2
    chunk_rows = -(-rows_total // (chunks * 16)) * 16
    padded_rows = chunk_rows * chunks

    def by_quarter(term):
        term = term.reshape(27, quarters, share, lanes)
        term = jnp.transpose(term, (1, 0, 2, 3)).reshape(quarters, rows_total, lanes)
        return jnp.pad(term, ((0, 0), (0, padded_rows - rows_total), (0, 0)))

    stacked = jnp.stack([by_quarter(first_local), by_quarter(down_local)], axis=1)
    gathered = reduce_gradients(stacked).reshape(2, padded_rows, lanes)[:, :rows_total]
    kernel_shape = (3, 3, 3, share, lanes)
    summed_first = gathered[0].reshape(kernel_shape)
    summed_down = gathered[1].reshape(kernel_shape)
    return (encoded[None], summed_first, summed_down)


def swap(value, axis, bit):
    return lax.ppermute(value, axis, [(i, i ^ bit) for i in range(lax.axis_size(axis))])


def ring_mask(bit, low_bits):
    return bit if bit in low_bits else bit | bit // 2


def swap_rows(value, bits, low_bits):
    count = lax.axis_size("height")
    pairs = []
    for group in range(lax.axis_size("dp")):
        mask = ring_mask(bits[group % 2], low_bits)
        pairs += [(group * count + i, group * count + (i ^ mask)) for i in range(count)]
    return lax.ppermute(value, ("dp", "height"), pairs)


def kept_bit(row, bit, low_bits):
    if bit in low_bits:
        return ((row // bit) ^ (row // (2 * bit))) % 2
    return (row // bit) % 2


def bits_of(count):
    return [1 << k for k in range(count.bit_length() - 1)]


def split_bit(blocks, names, name, high):
    place = names.index(name)
    mine = lax.dynamic_index_in_dim(blocks, high, place, keepdims=False)
    other = lax.dynamic_index_in_dim(blocks, 1 - high, place, keepdims=False)
    return mine, other, names[:place] + names[place + 1 :]


def reduce_gradients(stacked):
    dp_bits = bits_of(lax.axis_size("dp"))
    row_bits = bits_of(lax.axis_size("height"))
    frame_bits = bits_of(lax.axis_size("tm"))
    names = [("dp", bit) for bit in reversed(dp_bits)] + [("height", bit) for bit in reversed(row_bits)]
    blocks = stacked.reshape((2,) * len(names) + (-1, 128))
    for bit in dp_bits[:-1]:
        high = (lax.axis_index("dp") // bit) % 2
        mine, other, names = split_bit(blocks, names, ("dp", bit), high)
        blocks = mine + swap(other, "dp", bit)
    near = row_bits[0::2] + row_bits[1::2]
    crossed = [near[k ^ 1] if (k ^ 1) < len(near) else near[k] for k in range(len(near))]
    stages = list(zip(near, crossed))
    core = lax.axis_index("dp") % 2
    row = lax.axis_index("height")
    held = [names, names]
    low_bits = row_bits[0::2]
    for bits in stages:
        parts = []
        for variant in (0, 1):
            high = kept_bit(row, bits[variant], low_bits)
            mine, other, held[variant] = split_bit(blocks, held[variant], ("height", bits[variant]), high)
            parts.append((mine, other))
        mine = jnp.where(core == 0, parts[0][0], parts[1][0])
        other = jnp.where(core == 0, parts[0][1], parts[1][1])
        blocks = mine + swap_rows(other, bits, low_bits)
    far = dp_bits[-1]
    high = (lax.axis_index("dp") // far) % 2
    mine, other, _ = split_bit(blocks, held[0], ("dp", far), high)
    blocks = mine + swap(other, "dp", far)
    for bit in frame_bits:
        blocks = blocks + swap(blocks, "tm", bit)
    piece = blocks.astype(jnp.bfloat16)
    gathered = lax.all_gather(piece, "height", axis=0, tiled=False)
    owner = [h ^ sum((h >> 1) & bit for bit in low_bits) for h in range(gathered.shape[0])]
    return gathered[np.array(owner)]


def solution(mesh):
    in_specs = (
        P("dp", "tm", "height", None, None),
        P("dp", None),
        P(),
        P(),
        P("dp", "tm", "height", None, None),
    )
    out_specs = (
        P("dp", "tm", "height", None, None),
        P(None, None, None, "dp", None),
        P(None, None, None, "dp", None),
    )
    return jax.shard_map(body, mesh=mesh, in_specs=in_specs, out_specs=out_specs, check_vma=False)
```
